128 devices in a mesh: cell: 32 (over y, z, core), own: 4 (over x).
Axes of the slice: x: 4, y: 4, z: 4, core: 2. Of those that a mesh axis runs over, the one named last changes fastest.
Arguments:
- hist: bfloat16 [262144, 3, 256], P(('cell', 'own')), as said below
- dest: int32 [262144, 1], P(('cell', 'own')), may hold values from 0 to 127; in each aligned block of 2048 rows (0 to 2047, 2048 to 4095, ...) at most 32 rows name the same one
- cell_in: int32 [262144], P(('cell', 'own')), may hold values from 0 to 1023
- offsets: int32 [4, 131072], P(None, ('cell', 'own')), may hold values from -4 to 4
Outputs:
- multipliers: float32 [2, 6, 131072], P(None, None, ('cell', 'own'))
- fit_stat: float32 [2, 131072], P(None, ('cell', 'own'))
The draws below stay inside these ranges and needn't reach their ends.
Inputs may be any that keep to these rules, and one draw needn't show every extreme that they name: `dest`: the rows of one device name each cell block at most 32 times, and in every draw some device names some block exactly 32 times. `hist`: Positive, every entry at least three ten-thousandths of its row's largest.
All inputs are finite; a program needn't handle non-finite values.
Results may differ from the reference program's by a relative error of at most 0.0022.
Values may be sent and summed in bfloat16 or wider, within the bound.
No kernel may reach another device: no remote copies, remote signals or barrier semaphores. Data moves between devices by JAX's collectives and lax.ppermute only.
A program may use at most 64 MiB of HBM per device.

```python
import math
import jax
import jax.numpy as jnp
import numpy as np
from jax import lax

LEV = 128
SPEC = 2
REPL = 3
MOM = 6
NEWTON = 8
NEIGH = 4
W = 4
CB = 1024
ROWS = 2048
NCELL = 131072
ROWS_ALL = 262144
CAP = 32
DEVICES = 128


def draw_hist(key, part):
    key_rate = jax.random.fold_in(key, 11)
    key_rough = jax.random.fold_in(key, 12)
    key_scale = jax.random.fold_in(key, 13)
    log_rate = jax.random.uniform(key_rate, (ROWS_ALL, REPL, SPEC, 1), jnp.float32, jnp.log(0.3), jnp.log(2.5))
    rate = jnp.exp(log_rate)
    xpos = (2.0 * jnp.arange(LEV, dtype=jnp.float32) + 1.0) / LEV - 1.0
    shape = jnp.exp(-rate * (xpos[None, None, None, :] + 1.0))
    rough = jnp.exp(jax.random.uniform(key_rough, (ROWS_ALL, REPL, SPEC, LEV), jnp.float32, jnp.log(1.0 / 3.0), jnp.log(3.0)))
    scale = jnp.exp(jax.random.uniform(key_scale, (ROWS_ALL, 1, 1, 1), jnp.float32, 0.0, jnp.log(10.0)))
    values = shape * rough * scale
    return values.reshape(ROWS_ALL, REPL, SPEC * LEV).astype(jnp.bfloat16)


def place_ends(values, stream_key, smallest, top_value):
    shape = values.shape
    place = [jax.random.randint(jax.random.fold_in(stream_key, axis), (), 0, shape[axis]) for axis in range(len(shape))]
    values = values.at[tuple(place)].set(smallest)
    longest = shape.index(max(shape))
    place[longest] = (place[longest] + 1) % shape[longest]
    return values.at[tuple(place)].set(top_value)


def deal_out(key, own, number, rows, amount, top, reach, slope):
    sequence = jax.random.permutation(key, amount)
    crowded, usual = portions_of(amount, rows * top, reach, slope, True), portions_of(amount, rows * top, reach, slope, False)
    places = jnp.arange(amount)

    def named(tallies, rotation):
        used = int((tallies > 0).sum())
        fixed = max(1, used // 4)
        moved = fixed + (places - fixed + rotation * (used - fixed)) % max(1, amount - fixed)
        return jnp.zeros((amount,), jnp.int32).at[sequence[jnp.where(places < fixed, places, moved)]].set(jnp.asarray(tallies, jnp.int32))

    tallies = jnp.where(number % 4 == 0, named(crowded, number // 4), named(usual, number - number // 4 - 1))
    mixed = jax.random.permutation(jax.random.fold_in(own, 3), amount)
    donor, receiver = mixed[0:amount // 2 * 2:2], mixed[1:amount // 2 * 2:2]
    slack = jnp.minimum(tallies[donor] - 1, reach - tallies[receiver]) // 2
    slack = jnp.where((donor == sequence[0]) | (receiver == sequence[0]) | (tallies[receiver] == 0), 0, jnp.maximum(slack, 0))
    moved = jax.random.randint(jax.random.fold_in(own, 4), (amount // 2,), 0, 1 << 20) % (slack + 1)
    tallies = tallies.at[donor].add(-moved).at[receiver].add(moved)
    items = jnp.searchsorted(jnp.cumsum(tallies), jnp.arange(rows * top), side="right").astype(jnp.int32)
    grid = items.reshape(top, rows).T
    grid = grid[jax.random.permutation(jax.random.fold_in(own, 1), rows)]
    rotation = jax.random.randint(jax.random.fold_in(own, 2), (rows, 1), 0, top)
    return jnp.take_along_axis(grid, (jnp.arange(top)[None, :] + rotation) % top, axis=1)


def portions_of(number_of, total, limit, skew, full):
    loads = [(1 << 20) // math.isqrt(grade ** skew) + 1 for grade in range(1, number_of + 1)]
    largest = limit if full else min(limit, max(-(-total // number_of), total * loads[0] // sum(loads)))
    least = 1 if total - largest >= number_of - 1 else 0
    holding, rest = [largest] + [least] * (number_of - 1), total - largest - least * (number_of - 1)
    while rest > 0:
        free = [i for i in range(1, number_of) if holding[i] < largest] or [i for i in range(1, number_of) if holding[i] < limit]
        whole, remaining = sum([loads[i] for i in free]), rest
        for i in free:
            more = min(limit - holding[i], max(1, remaining * loads[i] // whole), rest)
            holding[i] = holding[i] + more
            rest = rest - more
    return np.array(holding)


def setup_inputs(seed: int = 0) -> dict:
    seeds = jax.random.split(jax.random.key(seed), 5)
    hist = draw_hist(jax.random.fold_in(seeds[4], 71), 0)
    dest_keys = jax.random.split(jax.random.fold_in(seeds[1], 1), ROWS_ALL // ROWS)
    dest_turns = jax.random.permutation(jax.random.fold_in(seeds[1], 3), ROWS_ALL // ROWS)
    dest = jax.vmap(lambda own, number: deal_out(jax.random.fold_in(seeds[1], 2), own, number, ROWS, DEVICES, 1, CAP, 2))(dest_keys, dest_turns).reshape((ROWS_ALL, 1))
    cell_in = place_ends(jax.random.randint(seeds[2], (ROWS_ALL,), 0, CB), jax.random.fold_in(seeds[2], 1), 0, CB - 1).astype(jnp.int32)
    offsets = place_ends(jax.random.randint(seeds[3], (NEIGH, NCELL), 0 - W, W + 1), jax.random.fold_in(seeds[3], 1), 0 - W, W).astype(jnp.int32)
    return dict(hist=hist, dest=dest, cell_in=cell_in, offsets=offsets)


def legendre_table(levels, count):
    xpos = (2.0 * jnp.arange(levels, dtype=jnp.float32) + 1.0) / levels - 1.0
    prev = jnp.ones_like(xpos)
    curr = xpos
    table = [curr]
    for order in range(1, count):
        nxt = ((2 * order + 1) * xpos * curr - order * prev) / (order + 1)
        prev, curr = (curr, nxt)
        table.append(curr)
    return jnp.stack(table, axis=0)

def chol_solve(hess, rhs, count):
    lower = [[None] * count for _ in range(count)]
    for row in range(count):
        for col in range(row + 1):
            total = hess[:, row, col]
            for inner in range(col):
                total = total - lower[row][inner] * lower[col][inner]
            if row == col:
                lower[row][col] = jnp.sqrt(total)
            else:
                lower[row][col] = total / lower[col][col]
    forward = []
    for row in range(count):
        total = rhs[:, row]
        for inner in range(row):
            total = total - lower[row][inner] * forward[inner]
        forward.append(total / lower[row][row])
    backward = [None] * count
    for row in reversed(range(count)):
        total = forward[row]
        for inner in range(row + 1, count):
            total = total - lower[inner][row] * backward[inner]
        backward[row] = total / lower[row][row]
    return jnp.stack(backward, axis=1)

def fit_entropy(target, count, steps):
    spec, levels, cells = target.shape
    hp = lax.Precision.HIGHEST
    phi = legendre_table(levels, count)
    psi = (phi[:, None, :] * phi[None, :, :]).reshape(count * count, levels)
    weights = target / lax.optimization_barrier(jnp.sum(target, axis=1, keepdims=True))
    moments = jnp.einsum('ml,slc->smc', phi, weights, precision=hp)
    lam = jnp.zeros((spec, count, cells), jnp.float32)
    ident = jnp.eye(count, dtype=jnp.float32)[None, :, :, None]
    for step in range(steps):
        expo = jnp.exp(jnp.einsum('ml,smc->slc', phi, lam, precision=hp))
        prob = expo / lax.optimization_barrier(jnp.sum(expo, axis=1, keepdims=True))
        first = jnp.einsum('ml,slc->smc', phi, prob, precision=hp)
        second = jnp.einsum('nl,slc->snc', psi, prob, precision=hp).reshape(spec, count, count, cells)
        hess = second - first[:, :, None, :] * first[:, None, :, :] + 0.01 * ident
        lam = lam - 0.5 * chol_solve(hess, first - moments, count)
    return lam

def fit_statistic(target, lam, count):
    spec, levels, cells = target.shape
    phi = legendre_table(levels, count)
    exponent = jnp.einsum('ml,smc->slc', phi, lam, precision=lax.Precision.HIGHEST)
    log_norm = jnp.log(lax.optimization_barrier(jnp.sum(jnp.exp(exponent), axis=1, keepdims=True)))
    total = lax.optimization_barrier(jnp.sum(target, axis=1, keepdims=True))
    ratio = jnp.log(target / total) - (exponent - log_norm)
    return 2.0 * lax.optimization_barrier(jnp.sum(target * ratio, axis=1)) / levels

def smooth_levels(field):
    padded = jnp.pad(field, ((0, 0), (1, 1), (0, 0)))
    return 0.5 * field + 0.25 * (padded[:, :-2, :] + padded[:, 2:, :])

def reference(hist, dest, cell_in, offsets):
    packed = lax.optimization_barrier(jnp.sum(hist.astype(jnp.float32), axis=1)).astype(jnp.bfloat16)
    cell_id = (dest[:, 0] * CB + cell_in).astype(jnp.int32)
    summed = jax.ops.segment_sum(packed.astype(jnp.float32), cell_id, num_segments=NCELL)
    cellhist = summed.T.reshape(SPEC, LEV, NCELL)
    levelled = smooth_levels(cellhist)
    padded = jnp.pad(levelled, ((0, 0), (0, 0), (W, W)))
    base = jnp.arange(NCELL, dtype=jnp.int32) + W
    target = 1.0 + levelled
    for j in range(NEIGH):
        target = target + jnp.take(padded, (base + offsets[j]).astype(jnp.int32), axis=2)
    lam = fit_entropy(target, MOM, NEWTON)
    return (lam, fit_statistic(target, lam, MOM))
```

```python
import jax
import jax.numpy as jnp
from jax import lax
from jax.experimental import pallas as pl
from jax.experimental.pallas import tpu as pltpu
from jax.sharding import PartitionSpec as P

SPEC = 2
MOM = 6
NEWTON = 8
NEIGH = 4
W = 4
CODE = 32
EXTRA = 8


def with_halo(block, sides, width):
    for axis, dim in sides:
        count = lax.axis_size(axis)
        forward = [(i, i + 1) for i in range(count - 1)]
        backward = [(target, source) for source, target in forward]
        low = lax.ppermute(
            lax.slice_in_dim(block, block.shape[dim] - width, None, axis=dim), axis, forward
        )
        high = lax.ppermute(lax.slice_in_dim(block, 0, width, axis=dim), axis, backward)
        block = jnp.concatenate([low, block, high], axis=dim)
    return block


def legendre_table(levels, count):
    xpos = (2.0 * jnp.arange(levels, dtype=jnp.float32) + 1.0) / levels - 1.0
    prev = jnp.ones_like(xpos)
    curr = xpos
    table = [curr]
    for order in range(1, count):
        nxt = ((2 * order + 1) * xpos * curr - order * prev) / (order + 1)
        prev, curr = (curr, nxt)
        table.append(curr)
    return jnp.stack(table, axis=0)


def pair_list(count):
    return [(row, col) for row in range(count) for col in range(row + 1)]


def chol_solve(hess, rhs, count):
    lower = [[None] * count for _ in range(count)]
    for row in range(count):
        for col in range(row + 1):
            total = hess[row][col]
            for inner in range(col):
                total = total - lower[row][inner] * lower[col][inner]
            if row == col:
                lower[row][col] = jnp.sqrt(total)
            else:
                lower[row][col] = total / lower[col][col]
    forward = []
    for row in range(count):
        total = rhs[row]
        for inner in range(row):
            total = total - lower[row][inner] * forward[inner]
        forward.append(total / lower[row][row])
    backward = [None] * count
    for row in reversed(range(count)):
        total = forward[row]
        for inner in range(row + 1, count):
            total = total - lower[inner][row] * backward[inner]
        backward[row] = total / lower[row][row]
    return backward


def fit_kernel(t_ref, phit_ref, psi_ref, lam_ref, fit_ref, lam_s):
    spec, levels, cells = t_ref.shape
    count = lam_ref.shape[1]
    highest = lax.Precision.HIGHEST
    pairs = pair_list(count)
    phit = phit_ref[...]
    psi = psi_ref[...]

    def contract(a, b):
        return jnp.dot(a, b, precision=highest, preferred_element_type=jnp.float32)

    for s in range(spec):
        target = t_ref[s]
        got = contract(psi, target)
        total = got[count : count + 1]
        moments = [got[m : m + 1] / total for m in range(count)]
        lam_s[...] = jnp.zeros(lam_s.shape, jnp.float32)
        lam = [jnp.zeros((1, cells), jnp.float32) for _ in range(count)]
        for step in range(NEWTON):
            expo = jnp.exp(contract(phit, lam_s[...]))
            got = contract(psi, expo)
            norm = got[count : count + 1]
            first = [got[m : m + 1] / norm for m in range(count)]
            hess = [[None] * count for _ in range(count)]
            for k, (row, col) in enumerate(pairs):
                second = got[count + 1 + k : count + 2 + k] / norm
                value = second - first[row] * first[col]
                if row == col:
                    value = value + 0.01
                hess[row][col] = value
            rhs = [first[m] - moments[m] for m in range(count)]
            delta = chol_solve(hess, rhs, count)
            for m in range(count):
                lam[m] = lam[m] - 0.5 * delta[m]
                lam_s[m : m + 1, :] = lam[m]
        exponent = contract(phit, lam_s[...])
        log_norm = jnp.log(jnp.sum(jnp.exp(exponent), axis=0, keepdims=True))
        whole = jnp.sum(target, axis=0, keepdims=True)
        ratio = jnp.log(target / whole) - (exponent - log_norm)
        fit_ref[s : s + 1, :] = 2.0 * jnp.sum(target * ratio, axis=0, keepdims=True) / levels
        lam_ref[s] = lam_s[0:count, :]


def fit_all(target, count):
    spec, levels, cells = target.shape
    phi = legendre_table(levels, count)
    pairs = pair_list(count)
    width = 8
    phit = jnp.zeros((levels, width), jnp.float32).at[:, :count].set(phi.T)
    rows = [phi[m] for m in range(count)] + [jnp.ones((levels,), jnp.float32)]
    rows += [phi[r] * phi[c] for r, c in pairs]
    height = -(-len(rows) // 8) * 8
    rows += [jnp.zeros((levels,), jnp.float32)] * (height - len(rows))
    psi = jnp.stack(rows, axis=0)
    return pl.pallas_call(
        fit_kernel,
        out_shape=(
            jax.ShapeDtypeStruct((spec, count, cells), jnp.float32),
            jax.ShapeDtypeStruct((spec, cells), jnp.float32),
        ),
        scratch_shapes=[pltpu.VMEM((width, cells), jnp.float32)],
    )(target, phit, psi)


def smooth_levels(field):
    padded = jnp.pad(field, ((0, 0), (1, 1), (0, 0)))
    return 0.5 * field + 0.25 * (padded[:, :-2, :] + padded[:, 2:, :])


def body(hist, dest, cell_in, offsets):
    rows = hist.shape[0]
    width = hist.shape[2]
    cells = offsets.shape[1]
    devices = lax.axis_size(("cell", "own"))
    capacity = 2 * rows // devices
    slots = devices * capacity
    packed = jnp.sum(hist, axis=1, dtype=jnp.float32).astype(jnp.bfloat16)
    target_block = dest[:, 0]
    member = (target_block[:, None] == jnp.arange(devices, dtype=jnp.int32)[None, :]).astype(
        jnp.int32
    )
    ranks = jnp.sum((jnp.cumsum(member, axis=0) - 1) * member, axis=1)
    position = target_block * capacity + ranks
    codes = jnp.stack([cell_in // CODE + 1, cell_in % CODE], axis=1).astype(jnp.bfloat16)
    codes = jnp.pad(codes, ((0, 0), (0, 128 - 2)))
    payload = jnp.concatenate([packed, codes], axis=1)
    place = (jnp.arange(slots, dtype=jnp.int32)[:, None] == position[None, :]).astype(jnp.bfloat16)
    sent = jnp.dot(place, payload, preferred_element_type=jnp.float32)
    send_rows = sent[:, :width].astype(jnp.bfloat16).reshape(devices, capacity, width)
    code_rows = sent[:, width : width + 2].reshape(devices, capacity, 2)
    code_rows = jnp.swapaxes(code_rows, 1, 2).astype(jnp.bfloat16)
    code_rows = jnp.pad(code_rows, ((0, 0), (0, EXTRA - 2), (0, width - capacity)))
    message = jnp.concatenate([send_rows, code_rows], axis=1)
    got = lax.all_to_all(message, ("cell", "own"), split_axis=0, concat_axis=0, tiled=True)
    recv_rows = got[:, :capacity, :].reshape(slots, width)
    high = got[:, capacity, :capacity].astype(jnp.int32).reshape(slots)
    low = got[:, capacity + 1, :capacity].astype(jnp.int32).reshape(slots)
    recv_cells = jnp.where(high > 0, (high - 1) * CODE + low, -1)
    select = (recv_cells[:, None] == jnp.arange(cells, dtype=jnp.int32)[None, :]).astype(
        jnp.bfloat16
    )
    summed = lax.dot_general(
        recv_rows, select, (((0,), (0,)), ((), ())), preferred_element_type=jnp.float32
    )
    cellhist = summed.reshape(SPEC, width // SPEC, cells)
    levelled = smooth_levels(cellhist)
    rimmed = with_halo(levelled, ((("cell", "own"), 2),), W)
    target = 1.0 + levelled
    for shift in range(-W, W + 1):
        weight = jnp.sum((offsets == shift).astype(jnp.float32), axis=0)
        target = target + weight[None, None, :] * lax.slice_in_dim(
            rimmed, W + shift, W + shift + cells, axis=2
        )
    return fit_all(target, MOM)


def solution(mesh):
    placed = (
        P(("cell", "own"), None, None),
        P(("cell", "own"), None),
        P(("cell", "own")),
        P(None, ("cell", "own")),
    )
    return jax.shard_map(
        body,
        mesh=mesh,
        in_specs=placed,
        out_specs=(P(None, None, ("cell", "own")), P(None, ("cell", "own"))),
        check_vma=False,
    )
```

```python
import jax
import jax.numpy as jnp
import numpy as np
from jax import lax
from jax.experimental import pallas as pl
from jax.experimental.pallas import tpu as pltpu
from jax.sharding import PartitionSpec as P

SPEC = 2
MOM = 6
NEWTON = 8
NEIGH = 4
W = 4
CODE = 32
EXTRA = 8


def with_halo(block, sides, width):
    for axis, dim in sides:
        count = lax.axis_size(axis)
        forward = [(i, i + 1) for i in range(count - 1)]
        backward = [(target, source) for source, target in forward]
        low = lax.ppermute(
            lax.slice_in_dim(block, block.shape[dim] - width, None, axis=dim), axis, forward
        )
        high = lax.ppermute(lax.slice_in_dim(block, 0, width, axis=dim), axis, backward)
        block = jnp.concatenate([low, block, high], axis=dim)
    return block


def legendre_table(levels, count):
    xpos = (2.0 * jnp.arange(levels, dtype=jnp.float32) + 1.0) / levels - 1.0
    prev = jnp.ones_like(xpos)
    curr = xpos
    table = [curr]
    for order in range(1, count):
        nxt = ((2 * order + 1) * xpos * curr - order * prev) / (order + 1)
        prev, curr = (curr, nxt)
        table.append(curr)
    return jnp.stack(table, axis=0)


def pair_list(count):
    return [(row, col) for row in range(count) for col in range(row + 1)]


def chol_solve(hess, rhs, count):
    lower = [[None] * count for _ in range(count)]
    for row in range(count):
        for col in range(row + 1):
            total = hess[row][col]
            for inner in range(col):
                total = total - lower[row][inner] * lower[col][inner]
            if row == col:
                lower[row][col] = jnp.sqrt(total)
            else:
                lower[row][col] = total / lower[col][col]
    forward = []
    for row in range(count):
        total = rhs[row]
        for inner in range(row):
            total = total - lower[row][inner] * forward[inner]
        forward.append(total / lower[row][row])
    backward = [None] * count
    for row in reversed(range(count)):
        total = forward[row]
        for inner in range(row + 1, count):
            total = total - lower[inner][row] * backward[inner]
        backward[row] = total / lower[row][row]
    return backward


def newton_step(got, moments, lam, count):
    pairs = pair_list(count)
    norm = got[count : count + 1]
    first = [got[m : m + 1] / norm for m in range(count)]
    hess = [[None] * count for _ in range(count)]
    for k, (row, col) in enumerate(pairs):
        second = got[count + 1 + k : count + 2 + k] / norm
        value = second - first[row] * first[col]
        if row == col:
            value = value + 0.01
        hess[row][col] = value
    rhs = [first[m] - moments[m] for m in range(count)]
    delta = chol_solve(hess, rhs, count)
    return [lam[m : m + 1] - 0.5 * delta[m] for m in range(count)]


def fit_kernel(t_ref, phit_ref, psi_ref, lam_ref, fit_ref, lam_s):
    spec, levels, cells = t_ref.shape
    count = lam_ref.shape[1]
    highest = lax.Precision.HIGHEST

    def contract(a, b):
        return jnp.dot(a, b, precision=highest, preferred_element_type=jnp.float32)

    moments = []
    for s in range(spec):
        got = contract(psi_ref[...], t_ref[s])
        total = got[count : count + 1]
        moments.append([got[m : m + 1] / total for m in range(count)])
    lam_s[...] = jnp.zeros(lam_s.shape, jnp.float32)

    def step(_, carry):
        for s in range(spec):
            lam = lam_s[s]
            expo = jnp.exp(contract(phit_ref[...], lam))
            got = contract(psi_ref[...], expo)
            new = newton_step(got, moments[s], lam, count)
            for m in range(count):
                lam_s[s, m : m + 1, :] = new[m]
        return carry

    lax.fori_loop(0, NEWTON, step, 0)
    for s in range(spec):
        target = t_ref[s]
        exponent = contract(phit_ref[...], lam_s[s])
        log_norm = jnp.log(jnp.sum(jnp.exp(exponent), axis=0, keepdims=True))
        whole = jnp.sum(target, axis=0, keepdims=True)
        ratio = jnp.log(target / whole) - (exponent - log_norm)
        fit_ref[s : s + 1, :] = 2.0 * jnp.sum(target * ratio, axis=0, keepdims=True) / levels
        lam_ref[s] = lam_s[s, 0:count, :]


def legendre_numpy(levels, count):
    xpos = (2.0 * np.arange(levels, dtype=np.float64) + 1.0) / levels - 1.0
    prev = np.ones_like(xpos)
    curr = xpos
    table = [curr]
    for order in range(1, count):
        nxt = ((2 * order + 1) * xpos * curr - order * prev) / (order + 1)
        prev, curr = (curr, nxt)
        table.append(curr)
    return np.stack(table, axis=0).astype(np.float32)


def fit_all(target, count):
    spec, levels, cells = target.shape
    phi = legendre_numpy(levels, count)
    pairs = pair_list(count)
    width = 8
    phit = np.zeros((levels, width), np.float32)
    phit[:, :count] = phi.T
    rows = [phi[m] for m in range(count)] + [np.ones((levels,), np.float32)]
    rows += [phi[r] * phi[c] for r, c in pairs]
    height = -(-len(rows) // 8) * 8
    rows += [np.zeros((levels,), np.float32)] * (height - len(rows))
    psi = np.stack(rows, axis=0)
    return pl.pallas_call(
        fit_kernel,
        out_shape=(
            jax.ShapeDtypeStruct((spec, count, cells), jnp.float32),
            jax.ShapeDtypeStruct((spec, cells), jnp.float32),
        ),
        scratch_shapes=[pltpu.VMEM((spec, width, cells), jnp.float32)],
    )(target, jnp.asarray(phit), jnp.asarray(psi))


def smooth_levels(field):
    padded = jnp.pad(field, ((0, 0), (1, 1), (0, 0)))
    return 0.5 * field + 0.25 * (padded[:, :-2, :] + padded[:, 2:, :])


def body(hist, dest, cell_in, offsets):
    rows = hist.shape[0]
    width = hist.shape[2]
    cells = offsets.shape[1]
    devices = lax.axis_size(("cell", "own"))
    capacity = 2 * rows // devices
    slots = devices * capacity
    packed = jnp.sum(hist, axis=1, dtype=jnp.float32).astype(jnp.bfloat16)
    target_block = dest[:, 0]
    member = (target_block[:, None] == jnp.arange(devices, dtype=jnp.int32)[None, :]).astype(
        jnp.int32
    )
    ranks = jnp.sum((jnp.cumsum(member, axis=0) - 1) * member, axis=1)
    position = target_block * capacity + ranks
    codes = jnp.stack([cell_in // CODE + 1, cell_in % CODE], axis=1).astype(jnp.bfloat16)
    codes = jnp.pad(codes, ((0, 0), (0, 128 - 2)))
    payload = jnp.concatenate([packed, codes], axis=1)
    place = (jnp.arange(slots, dtype=jnp.int32)[:, None] == position[None, :]).astype(jnp.bfloat16)
    sent = jnp.dot(place, payload, preferred_element_type=jnp.float32)
    send_rows = sent[:, :width].astype(jnp.bfloat16).reshape(devices, capacity, width)
    code_rows = sent[:, width : width + 2].reshape(devices, capacity, 2)
    code_rows = jnp.swapaxes(code_rows, 1, 2).astype(jnp.bfloat16)
    code_rows = jnp.pad(code_rows, ((0, 0), (0, EXTRA - 2), (0, width - capacity)))
    message = jnp.concatenate([send_rows, code_rows], axis=1)
    got = lax.all_to_all(message, ("cell", "own"), split_axis=0, concat_axis=0, tiled=True)
    recv_rows = got[:, :capacity, :].reshape(slots, width)
    high = got[:, capacity, :capacity].astype(jnp.int32).reshape(slots)
    low = got[:, capacity + 1, :capacity].astype(jnp.int32).reshape(slots)
    recv_cells = jnp.where(high > 0, (high - 1) * CODE + low, -1)
    select = (recv_cells[:, None] == jnp.arange(cells, dtype=jnp.int32)[None, :]).astype(
        jnp.bfloat16
    )
    summed = lax.dot_general(
        recv_rows, select, (((0,), (0,)), ((), ())), preferred_element_type=jnp.float32
    )
    cellhist = summed.reshape(SPEC, width // SPEC, cells)
    levelled = smooth_levels(cellhist)
    rimmed = with_halo(levelled, ((("cell", "own"), 2),), W)
    target = 1.0 + levelled
    for shift in range(-W, W + 1):
        weight = jnp.sum((offsets == shift).astype(jnp.float32), axis=0)
        target = target + weight[None, None, :] * lax.slice_in_dim(
            rimmed, W + shift, W + shift + cells, axis=2
        )
    return fit_all(target, MOM)


def solution(mesh):
    placed = (
        P(("cell", "own"), None, None),
        P(("cell", "own"), None),
        P(("cell", "own")),
        P(None, ("cell", "own")),
    )
    return jax.shard_map(
        body,
        mesh=mesh,
        in_specs=placed,
        out_specs=(P(None, None, ("cell", "own")), P(None, ("cell", "own"))),
        check_vma=False,
    )
```

```python
import jax
import jax.numpy as jnp
import numpy as np
from jax import lax
from jax.experimental import pallas as pl
from jax.experimental.pallas import tpu as pltpu
from jax.sharding import PartitionSpec as P

SPEC = 2
MOM = 6
NEWTON = 8
W = 4
CODE = 32
EXTRA = 8


def pair_list(count):
    return [(row, col) for row in range(count) for col in range(row + 1)]


def chol_solve(hess, rhs, count):
    lower = [[None] * count for _ in range(count)]
    for row in range(count):
        for col in range(row + 1):
            total = hess[row][col]
            for inner in range(col):
                total = total - lower[row][inner] * lower[col][inner]
            if row == col:
                lower[row][col] = jnp.sqrt(total)
            else:
                lower[row][col] = total / lower[col][col]
    forward = []
    for row in range(count):
        total = rhs[row]
        for inner in range(row):
            total = total - lower[row][inner] * forward[inner]
        forward.append(total / lower[row][row])
    backward = [None] * count
    for row in reversed(range(count)):
        total = forward[row]
        for inner in range(row + 1, count):
            total = total - lower[inner][row] * backward[inner]
        backward[row] = total / lower[row][row]
    return backward


def newton_step(got, moments, lam, count):
    pairs = pair_list(count)
    norm = got[count : count + 1]
    first = [got[m : m + 1] / norm for m in range(count)]
    hess = [[None] * count for _ in range(count)]
    for k, (row, col) in enumerate(pairs):
        second = got[count + 1 + k : count + 2 + k] / norm
        value = second - first[row] * first[col]
        if row == col:
            value = value + 0.01
        hess[row][col] = value
    rhs = [first[m] - moments[m] for m in range(count)]
    delta = chol_solve(hess, rhs, count)
    return [lam[m : m + 1] - 0.5 * delta[m] for m in range(count)]


def fit_kernel(t_ref, phit_ref, psi_ref, lam_ref, fit_ref, lam_s):
    spec, levels, _ = t_ref.shape
    count = lam_ref.shape[1]
    highest = lax.Precision.HIGHEST

    def contract(a, b):
        return jnp.dot(a, b, precision=highest, preferred_element_type=jnp.float32)

    moments = []
    for s in range(spec):
        got = contract(psi_ref[...], t_ref[s])
        total = got[count : count + 1]
        moments.append([got[m : m + 1] / total for m in range(count)])
    lam_s[...] = jnp.zeros(lam_s.shape, jnp.float32)

    def step(_, carry):
        for s in range(spec):
            lam = lam_s[s]
            expo = jnp.exp(contract(phit_ref[...], lam))
            got = contract(psi_ref[...], expo)
            new = newton_step(got, moments[s], lam, count)
            for m in range(count):
                lam_s[s, m : m + 1, :] = new[m]
        return carry

    lax.fori_loop(0, NEWTON, step, 0)
    for s in range(spec):
        target = t_ref[s]
        exponent = contract(phit_ref[...], lam_s[s])
        log_norm = jnp.log(jnp.sum(jnp.exp(exponent), axis=0, keepdims=True))
        whole = jnp.sum(target, axis=0, keepdims=True)
        ratio = jnp.log(target / whole) - (exponent - log_norm)
        fit_ref[s : s + 1, :] = 2.0 * jnp.sum(target * ratio, axis=0, keepdims=True) / levels
        lam_ref[s] = lam_s[s, 0:count, :]


def legendre_numpy(levels, count):
    xpos = (2.0 * np.arange(levels, dtype=np.float64) + 1.0) / levels - 1.0
    prev = np.ones_like(xpos)
    curr = xpos
    table = [curr]
    for order in range(1, count):
        nxt = ((2 * order + 1) * xpos * curr - order * prev) / (order + 1)
        prev, curr = (curr, nxt)
        table.append(curr)
    return np.stack(table, axis=0).astype(np.float32)


def fit_all(target, count):
    spec, levels, cells = target.shape
    phi = legendre_numpy(levels, count)
    pairs = pair_list(count)
    width = 8
    phit = np.zeros((levels, width), np.float32)
    phit[:, :count] = phi.T
    rows = [phi[m] for m in range(count)] + [np.ones((levels,), np.float32)]
    rows += [phi[r] * phi[c] for r, c in pairs]
    height = -(-len(rows) // 8) * 8
    rows += [np.zeros((levels,), np.float32)] * (height - len(rows))
    psi = np.stack(rows, axis=0)
    return pl.pallas_call(
        fit_kernel,
        out_shape=(
            jax.ShapeDtypeStruct((spec, count, cells), jnp.float32),
            jax.ShapeDtypeStruct((spec, cells), jnp.float32),
        ),
        scratch_shapes=[pltpu.VMEM((spec, width, cells), jnp.float32)],
    )(target, jnp.asarray(phit), jnp.asarray(psi))


def smooth_levels(field):
    padded = jnp.pad(field, ((0, 0), (1, 1), (0, 0)))
    return 0.5 * field + 0.25 * (padded[:, :-2, :] + padded[:, 2:, :])


def body_inner(hist, dest, cell_in, offsets):
    rows = hist.shape[0]
    width = hist.shape[2]
    cells = offsets.shape[1]
    devices = lax.axis_size(("cell", "own"))
    capacity = 2 * rows // devices
    slots = devices * capacity
    packed = jnp.sum(hist, axis=1, dtype=jnp.float32).astype(jnp.bfloat16)
    target_block = dest[:, 0]
    member = (target_block[:, None] == jnp.arange(devices, dtype=jnp.int32)[None, :]).astype(
        jnp.int32
    )
    ranks = jnp.sum((jnp.cumsum(member, axis=0) - 1) * member, axis=1)
    position = target_block * capacity + ranks
    codes = jnp.stack([cell_in // CODE + 1, cell_in % CODE], axis=1).astype(jnp.bfloat16)
    codes = jnp.pad(codes, ((0, 0), (0, 128 - 2)))
    payload = jnp.concatenate([packed, codes], axis=1)
    place = (jnp.arange(slots, dtype=jnp.int32)[:, None] == position[None, :]).astype(jnp.bfloat16)
    sent = jnp.dot(place, payload, preferred_element_type=jnp.float32)
    send_rows = sent[:, :width].astype(jnp.bfloat16).reshape(devices, capacity, width)
    code_rows = sent[:, width : width + 2].reshape(devices, capacity, 2)
    code_rows = jnp.swapaxes(code_rows, 1, 2).astype(jnp.bfloat16)
    code_rows = jnp.pad(code_rows, ((0, 0), (0, EXTRA - 2), (0, width - capacity)))
    message = jnp.concatenate([send_rows, code_rows], axis=1)
    got = lax.all_to_all(message, ("cell", "own"), split_axis=0, concat_axis=0, tiled=True)
    lanes = capacity + EXTRA
    recv_rows = got.reshape(devices * lanes, width)
    high = got[:, capacity, :capacity].astype(jnp.int32)
    low = got[:, capacity + 1, :capacity].astype(jnp.int32)
    recv_cells = jnp.where(high > 0, (high - 1) * CODE + low, -1)
    recv_cells = jnp.pad(recv_cells, ((0, 0), (0, EXTRA)), constant_values=-1).reshape(devices * lanes)
    edges = jnp.concatenate(
        [jnp.arange(W, dtype=jnp.int32), jnp.arange(cells - W, cells, dtype=jnp.int32)]
    )
    edge_select = (recv_cells[:, None] == edges[None, :]).astype(jnp.bfloat16)
    edge_sum = lax.dot_general(
        recv_rows, edge_select, (((0,), (0,)), ((), ())), preferred_element_type=jnp.float32
    )
    edge_lev = smooth_levels(edge_sum.reshape(SPEC, width // SPEC, 2 * W))
    count = devices
    forward = [(i, i + 1) for i in range(count - 1)]
    backward = [(target, source) for source, target in forward]
    below = lax.ppermute(edge_lev[:, :, W:], ("cell", "own"), forward)
    above = lax.ppermute(edge_lev[:, :, :W], ("cell", "own"), backward)
    select = (recv_cells[:, None] == jnp.arange(cells, dtype=jnp.int32)[None, :]).astype(
        jnp.bfloat16
    )
    summed = lax.dot_general(
        recv_rows, select, (((0,), (0,)), ((), ())), preferred_element_type=jnp.float32
    )
    cellhist = summed.reshape(SPEC, width // SPEC, cells)
    levelled = smooth_levels(cellhist)
    rimmed = jnp.concatenate([below, levelled, above], axis=2)
    target = 1.0 + levelled
    for shift in range(-W, W + 1):
        weight = jnp.sum((offsets == shift).astype(jnp.float32), axis=0)
        target = target + weight[None, None, :] * lax.slice_in_dim(
            rimmed, W + shift, W + shift + cells, axis=2
        )
    return fit_all(target, MOM)


def solution(mesh):
    placed = (
        P(("cell", "own"), None, None),
        P(("cell", "own"), None),
        P(("cell", "own")),
        P(None, ("cell", "own")),
    )
    return jax.shard_map(
        body_inner,
        mesh=mesh,
        in_specs=placed,
        out_specs=(P(None, None, ("cell", "own")), P(None, ("cell", "own"))),
        check_vma=False,
    )
```

```python
import jax
import jax.numpy as jnp
import numpy as np
from jax import lax
from jax.experimental import pallas as pl
from jax.experimental.pallas import tpu as pltpu
from jax.sharding import PartitionSpec as P

SPEC = 2
MOM = 6
NEWTON = 8
W = 4
CODE = 32
EXTRA = 8


def pair_list(count):
    return [(row, col) for row in range(count) for col in range(row + 1)]


def chol_solve(hess, rhs, count):
    lower = [[None] * count for _ in range(count)]
    for row in range(count):
        for col in range(row + 1):
            total = hess[row][col]
            for inner in range(col):
                total = total - lower[row][inner] * lower[col][inner]
            if row == col:
                lower[row][col] = jnp.sqrt(total)
            else:
                lower[row][col] = total / lower[col][col]
    forward = []
    for row in range(count):
        total = rhs[row]
        for inner in range(row):
            total = total - lower[row][inner] * forward[inner]
        forward.append(total / lower[row][row])
    backward = [None] * count
    for row in reversed(range(count)):
        total = forward[row]
        for inner in range(row + 1, count):
            total = total - lower[inner][row] * backward[inner]
        backward[row] = total / lower[row][row]
    return backward


def newton_step(got, moments, lam, count):
    pairs = pair_list(count)
    norm = got[count]
    first = [got[m] / norm for m in range(count)]
    hess = [[None] * count for _ in range(count)]
    for k, (row, col) in enumerate(pairs):
        second = got[count + 1 + k] / norm
        value = second - first[row] * first[col]
        if row == col:
            value = value + 0.01
        hess[row][col] = value
    rhs = [first[m] - moments[m] for m in range(count)]
    delta = chol_solve(hess, rhs, count)
    return [lam[m] - 0.5 * delta[m] for m in range(count)]


def fit_kernel(t_ref, phit_ref, psi_ref, lam_ref, fit_ref, lam_s, dense_ref):
    spec, levels, cells = t_ref.shape
    count = lam_ref.shape[1]
    used = count + 1 + len(pair_list(count))
    groups = 8 // spec
    part = cells // groups
    highest = lax.Precision.HIGHEST

    def contract(a, b):
        return jnp.dot(a, b, precision=highest, preferred_element_type=jnp.float32)

    def densify(gots):
        for s in range(spec):
            for j in range(groups):
                piece = gots[s][:, j * part : (j + 1) * part]
                row = s * groups + j
                for k in range(used):
                    dense_ref[k, row : row + 1, :] = piece[k : k + 1, :]
        return [dense_ref[k] for k in range(used)]

    def spread(values):
        for m in range(count):
            for s in range(spec):
                for j in range(groups):
                    row = s * groups + j
                    lam_s[s, m : m + 1, j * part : (j + 1) * part] = values[m][row : row + 1, :]

    got = densify([contract(psi_ref[...], t_ref[s]) for s in range(spec)])
    moments = [got[m] / got[count] for m in range(count)]
    lam_s[...] = jnp.zeros(lam_s.shape, jnp.float32)
    zero = jnp.zeros((8, part), jnp.float32)

    def step(_, lam):
        gots = []
        for s in range(spec):
            expo = jnp.exp(contract(phit_ref[...], lam_s[s]))
            gots.append(contract(psi_ref[...], expo))
        new = newton_step(densify(gots), moments, list(lam), count)
        spread(new)
        return tuple(new)

    lax.fori_loop(0, NEWTON, step, tuple([zero] * count))
    for s in range(spec):
        target = t_ref[s]
        exponent = contract(phit_ref[...], lam_s[s])
        log_norm = jnp.log(jnp.sum(jnp.exp(exponent), axis=0, keepdims=True))
        whole = jnp.sum(target, axis=0, keepdims=True)
        ratio = jnp.log(target / whole) - (exponent - log_norm)
        fit_ref[s : s + 1, :] = 2.0 * jnp.sum(target * ratio, axis=0, keepdims=True) / levels
        lam_ref[s] = lam_s[s, 0:count, :]


def legendre_numpy(levels, count):
    xpos = (2.0 * np.arange(levels, dtype=np.float64) + 1.0) / levels - 1.0
    prev = np.ones_like(xpos)
    curr = xpos
    table = [curr]
    for order in range(1, count):
        nxt = ((2 * order + 1) * xpos * curr - order * prev) / (order + 1)
        prev, curr = (curr, nxt)
        table.append(curr)
    return np.stack(table, axis=0).astype(np.float32)


def fit_all(target, count):
    spec, levels, cells = target.shape
    phi = legendre_numpy(levels, count)
    pairs = pair_list(count)
    width = 8
    phit = np.zeros((levels, width), np.float32)
    phit[:, :count] = phi.T
    rows = [phi[m] for m in range(count)] + [np.ones((levels,), np.float32)]
    rows += [phi[r] * phi[c] for r, c in pairs]
    height = -(-len(rows) // 8) * 8
    rows += [np.zeros((levels,), np.float32)] * (height - len(rows))
    psi = np.stack(rows, axis=0)
    return pl.pallas_call(
        fit_kernel,
        out_shape=(
            jax.ShapeDtypeStruct((spec, count, cells), jnp.float32),
            jax.ShapeDtypeStruct((spec, cells), jnp.float32),
        ),
        scratch_shapes=[
            pltpu.VMEM((spec, width, cells), jnp.float32),
            pltpu.VMEM((height, 8, cells * spec // 8), jnp.float32),
        ],
    )(target, jnp.asarray(phit), jnp.asarray(psi))


def smooth_levels(field):
    padded = jnp.pad(field, ((0, 0), (1, 1), (0, 0)))
    return 0.5 * field + 0.25 * (padded[:, :-2, :] + padded[:, 2:, :])


def body_inner(hist, dest, cell_in, offsets):
    rows = hist.shape[0]
    width = hist.shape[2]
    cells = offsets.shape[1]
    devices = lax.axis_size(("cell", "own"))
    capacity = 2 * rows // devices
    slots = devices * capacity
    packed = jnp.sum(hist, axis=1, dtype=jnp.float32).astype(jnp.bfloat16)
    target_block = dest[:, 0]
    member = (target_block[:, None] == jnp.arange(devices, dtype=jnp.int32)[None, :]).astype(
        jnp.int32
    )
    ranks = jnp.sum((jnp.cumsum(member, axis=0) - 1) * member, axis=1)
    position = target_block * capacity + ranks
    codes = jnp.stack([cell_in // CODE + 1, cell_in % CODE], axis=1).astype(jnp.bfloat16)
    codes = jnp.pad(codes, ((0, 0), (0, 128 - 2)))
    payload = jnp.concatenate([packed, codes], axis=1)
    place = (jnp.arange(slots, dtype=jnp.int32)[:, None] == position[None, :]).astype(jnp.bfloat16)
    sent = jnp.dot(place, payload, preferred_element_type=jnp.float32)
    send_rows = sent[:, :width].astype(jnp.bfloat16).reshape(devices, capacity, width)
    code_rows = sent[:, width : width + 2].reshape(devices, capacity, 2)
    code_rows = jnp.swapaxes(code_rows, 1, 2).astype(jnp.bfloat16)
    code_rows = jnp.pad(code_rows, ((0, 0), (0, EXTRA - 2), (0, width - capacity)))
    message = jnp.concatenate([send_rows, code_rows], axis=1)
    got = lax.all_to_all(message, ("cell", "own"), split_axis=0, concat_axis=0, tiled=True)
    lanes = capacity + EXTRA
    recv_rows = got.reshape(devices * lanes, width)
    high = got[:, capacity, :capacity].astype(jnp.int32)
    low = got[:, capacity + 1, :capacity].astype(jnp.int32)
    recv_cells = jnp.where(high > 0, (high - 1) * CODE + low, -1)
    recv_cells = jnp.pad(recv_cells, ((0, 0), (0, EXTRA)), constant_values=-1).reshape(devices * lanes)
    edges = jnp.concatenate(
        [jnp.arange(W, dtype=jnp.int32), jnp.arange(cells - W, cells, dtype=jnp.int32)]
    )
    edge_select = (recv_cells[:, None] == edges[None, :]).astype(jnp.bfloat16)
    edge_sum = lax.dot_general(
        recv_rows, edge_select, (((0,), (0,)), ((), ())), preferred_element_type=jnp.float32
    )
    edge_lev = smooth_levels(edge_sum.reshape(SPEC, width // SPEC, 2 * W))
    count = devices
    forward = [(i, i + 1) for i in range(count - 1)]
    backward = [(target, source) for source, target in forward]
    below = lax.ppermute(edge_lev[:, :, W:], ("cell", "own"), forward)
    above = lax.ppermute(edge_lev[:, :, :W], ("cell", "own"), backward)
    select = (recv_cells[:, None] == jnp.arange(cells, dtype=jnp.int32)[None, :]).astype(
        jnp.bfloat16
    )
    summed = lax.dot_general(
        recv_rows, select, (((0,), (0,)), ((), ())), preferred_element_type=jnp.float32
    )
    cellhist = summed.reshape(SPEC, width // SPEC, cells)
    levelled = smooth_levels(cellhist)
    rimmed = jnp.concatenate([below, levelled, above], axis=2)
    target = 1.0 + levelled
    for shift in range(-W, W + 1):
        weight = jnp.sum((offsets == shift).astype(jnp.float32), axis=0)
        target = target + weight[None, None, :] * lax.slice_in_dim(
            rimmed, W + shift, W + shift + cells, axis=2
        )
    return fit_all(target, MOM)


def solution(mesh):
    placed = (
        P(("cell", "own"), None, None),
        P(("cell", "own"), None),
        P(("cell", "own")),
        P(None, ("cell", "own")),
    )
    return jax.shard_map(
        body_inner,
        mesh=mesh,
        in_specs=placed,
        out_specs=(P(None, None, ("cell", "own")), P(None, ("cell", "own"))),
        check_vma=False,
    )
```

```python
import jax
import jax.numpy as jnp
import numpy as np
from jax import lax
from jax.experimental import pallas as pl
from jax.experimental.pallas import tpu as pltpu
from jax.sharding import PartitionSpec as P

SPEC = 2
MOM = 6
NEWTON = 8
W = 4
CODE = 32
EXTRA = 8
LOOP_PRECISION = lax.Precision.HIGH


def pair_list(count):
    return [(row, col) for row in range(count) for col in range(row + 1)]


def chol_solve(hess, rhs, count):
    lower = [[None] * count for _ in range(count)]
    for row in range(count):
        for col in range(row + 1):
            total = hess[row][col]
            for inner in range(col):
                total = total - lower[row][inner] * lower[col][inner]
            if row == col:
                lower[row][col] = jnp.sqrt(total)
            else:
                lower[row][col] = total / lower[col][col]
    forward = []
    for row in range(count):
        total = rhs[row]
        for inner in range(row):
            total = total - lower[row][inner] * forward[inner]
        forward.append(total / lower[row][row])
    backward = [None] * count
    for row in reversed(range(count)):
        total = forward[row]
        for inner in range(row + 1, count):
            total = total - lower[inner][row] * backward[inner]
        backward[row] = total / lower[row][row]
    return backward


def newton_step(got, moments, lam, count):
    pairs = pair_list(count)
    norm = got[count]
    first = [got[m] / norm for m in range(count)]
    hess = [[None] * count for _ in range(count)]
    for k, (row, col) in enumerate(pairs):
        second = got[count + 1 + k] / norm
        value = second - first[row] * first[col]
        if row == col:
            value = value + 0.01
        hess[row][col] = value
    rhs = [first[m] - moments[m] for m in range(count)]
    delta = chol_solve(hess, rhs, count)
    return [lam[m] - 0.5 * delta[m] for m in range(count)]


def fit_kernel(t_ref, phit_ref, psi_ref, lam_ref, fit_ref, lam_s, dense_ref):
    spec, levels, cells = t_ref.shape
    count = lam_ref.shape[1]
    used = count + 1 + len(pair_list(count))
    groups = 8 // spec
    part = cells // groups
    highest = lax.Precision.HIGHEST

    def contract(a, b, precision=highest):
        return jnp.dot(a, b, precision=precision, preferred_element_type=jnp.float32)

    def densify(gots):
        for s in range(spec):
            for j in range(groups):
                piece = gots[s][:, j * part : (j + 1) * part]
                row = s * groups + j
                for k in range(used):
                    dense_ref[k, row : row + 1, :] = piece[k : k + 1, :]
        return [dense_ref[k] for k in range(used)]

    def spread(values):
        for m in range(count):
            for s in range(spec):
                for j in range(groups):
                    row = s * groups + j
                    lam_s[s, m : m + 1, j * part : (j + 1) * part] = values[m][row : row + 1, :]

    got = densify([contract(psi_ref[...], t_ref[s]) for s in range(spec)])
    moments = [got[m] / got[count] for m in range(count)]
    lam_s[...] = jnp.zeros(lam_s.shape, jnp.float32)
    zero = jnp.zeros((8, part), jnp.float32)

    def step(_, lam):
        gots = []
        for s in range(spec):
            expo = jnp.exp(contract(phit_ref[...], lam_s[s], LOOP_PRECISION))
            gots.append(contract(psi_ref[...], expo, LOOP_PRECISION))
        new = newton_step(densify(gots), moments, list(lam), count)
        spread(new)
        return tuple(new)

    lax.fori_loop(0, NEWTON, step, tuple([zero] * count))
    for s in range(spec):
        target = t_ref[s]
        exponent = contract(phit_ref[...], lam_s[s])
        log_norm = jnp.log(jnp.sum(jnp.exp(exponent), axis=0, keepdims=True))
        whole = jnp.sum(target, axis=0, keepdims=True)
        ratio = jnp.log(target / whole) - (exponent - log_norm)
        fit_ref[s : s + 1, :] = 2.0 * jnp.sum(target * ratio, axis=0, keepdims=True) / levels
        lam_ref[s] = lam_s[s, 0:count, :]


def legendre_numpy(levels, count):
    xpos = (2.0 * np.arange(levels, dtype=np.float64) + 1.0) / levels - 1.0
    prev = np.ones_like(xpos)
    curr = xpos
    table = [curr]
    for order in range(1, count):
        nxt = ((2 * order + 1) * xpos * curr - order * prev) / (order + 1)
        prev, curr = (curr, nxt)
        table.append(curr)
    return np.stack(table, axis=0).astype(np.float32)


def fit_all(target, count):
    spec, levels, cells = target.shape
    phi = legendre_numpy(levels, count)
    pairs = pair_list(count)
    width = 8
    phit = np.zeros((levels, width), np.float32)
    phit[:, :count] = phi.T
    rows = [phi[m] for m in range(count)] + [np.ones((levels,), np.float32)]
    rows += [phi[r] * phi[c] for r, c in pairs]
    height = -(-len(rows) // 8) * 8
    rows += [np.zeros((levels,), np.float32)] * (height - len(rows))
    psi = np.stack(rows, axis=0)
    return pl.pallas_call(
        fit_kernel,
        out_shape=(
            jax.ShapeDtypeStruct((spec, count, cells), jnp.float32),
            jax.ShapeDtypeStruct((spec, cells), jnp.float32),
        ),
        scratch_shapes=[
            pltpu.VMEM((spec, width, cells), jnp.float32),
            pltpu.VMEM((height, 8, cells * spec // 8), jnp.float32),
        ],
    )(target, jnp.asarray(phit), jnp.asarray(psi))


def smooth_levels(field):
    padded = jnp.pad(field, ((0, 0), (1, 1), (0, 0)))
    return 0.5 * field + 0.25 * (padded[:, :-2, :] + padded[:, 2:, :])


def body_inner(hist, dest, cell_in, offsets):
    rows = hist.shape[0]
    width = hist.shape[2]
    cells = offsets.shape[1]
    devices = lax.axis_size(("cell", "own"))
    capacity = 2 * rows // devices
    slots = devices * capacity
    packed = jnp.sum(hist, axis=1, dtype=jnp.float32).astype(jnp.bfloat16)
    target_block = dest[:, 0]
    member = (target_block[:, None] == jnp.arange(devices, dtype=jnp.int32)[None, :]).astype(
        jnp.int32
    )
    ranks = jnp.sum((jnp.cumsum(member, axis=0) - 1) * member, axis=1)
    position = target_block * capacity + ranks
    codes = jnp.stack([cell_in // CODE + 1, cell_in % CODE], axis=1).astype(jnp.bfloat16)
    codes = jnp.pad(codes, ((0, 0), (0, 128 - 2)))
    payload = jnp.concatenate([packed, codes], axis=1)
    place = (jnp.arange(slots, dtype=jnp.int32)[:, None] == position[None, :]).astype(jnp.bfloat16)
    sent = jnp.dot(place, payload, preferred_element_type=jnp.float32)
    send_rows = sent[:, :width].astype(jnp.bfloat16).reshape(devices, capacity, width)
    code_rows = sent[:, width : width + 2].reshape(devices, capacity, 2)
    code_rows = jnp.swapaxes(code_rows, 1, 2).astype(jnp.bfloat16)
    code_rows = jnp.pad(code_rows, ((0, 0), (0, EXTRA - 2), (0, width - capacity)))
    message = jnp.concatenate([send_rows, code_rows], axis=1)
    got = lax.all_to_all(message, ("cell", "own"), split_axis=0, concat_axis=0, tiled=True)
    lanes = capacity + EXTRA
    recv_rows = got.reshape(devices * lanes, width)
    high = got[:, capacity, :capacity].astype(jnp.int32)
    low = got[:, capacity + 1, :capacity].astype(jnp.int32)
    recv_cells = jnp.where(high > 0, (high - 1) * CODE + low, -1)
    recv_cells = jnp.pad(recv_cells, ((0, 0), (0, EXTRA)), constant_values=-1).reshape(devices * lanes)
    edges = jnp.concatenate(
        [jnp.arange(W, dtype=jnp.int32), jnp.arange(cells - W, cells, dtype=jnp.int32)]
    )
    edge_select = (recv_cells[:, None] == edges[None, :]).astype(jnp.bfloat16)
    edge_sum = lax.dot_general(
        recv_rows, edge_select, (((0,), (0,)), ((), ())), preferred_element_type=jnp.float32
    )
    edge_lev = smooth_levels(edge_sum.reshape(SPEC, width // SPEC, 2 * W))
    count = devices
    forward = [(i, i + 1) for i in range(count - 1)]
    backward = [(target, source) for source, target in forward]
    below = lax.ppermute(edge_lev[:, :, W:], ("cell", "own"), forward)
    above = lax.ppermute(edge_lev[:, :, :W], ("cell", "own"), backward)
    select = (recv_cells[:, None] == jnp.arange(cells, dtype=jnp.int32)[None, :]).astype(
        jnp.bfloat16
    )
    summed = lax.dot_general(
        recv_rows, select, (((0,), (0,)), ((), ())), preferred_element_type=jnp.float32
    )
    cellhist = summed.reshape(SPEC, width // SPEC, cells)
    levelled = smooth_levels(cellhist)
    rimmed = jnp.concatenate([below, levelled, above], axis=2)
    target = 1.0 + levelled
    for shift in range(-W, W + 1):
        weight = jnp.sum((offsets == shift).astype(jnp.float32), axis=0)
        target = target + weight[None, None, :] * lax.slice_in_dim(
            rimmed, W + shift, W + shift + cells, axis=2
        )
    return fit_all(target, MOM)


def solution(mesh):
    placed = (
        P(("cell", "own"), None, None),
        P(("cell", "own"), None),
        P(("cell", "own")),
        P(None, ("cell", "own")),
    )
    return jax.shard_map(
        body_inner,
        mesh=mesh,
        in_specs=placed,
        out_specs=(P(None, None, ("cell", "own")), P(None, ("cell", "own"))),
        check_vma=False,
    )
```

```python
import jax
import jax.numpy as jnp
import numpy as np
from jax import lax
from jax.experimental import pallas as pl
from jax.experimental.pallas import tpu as pltpu
from jax.sharding import PartitionSpec as P

SPEC = 2
MOM = 6
NEWTON = 8
W = 4
CODE = 32
EXTRA = 8
LOOP_PRECISION = lax.Precision.HIGH


def pair_list(count):
    return [(row, col) for row in range(count) for col in range(row + 1)]


def chol_solve(hess, rhs, count):
    lower = [[None] * count for _ in range(count)]
    for row in range(count):
        for col in range(row + 1):
            total = hess[row][col]
            for inner in range(col):
                total = total - lower[row][inner] * lower[col][inner]
            if row == col:
                lower[row][col] = jnp.sqrt(total)
            else:
                lower[row][col] = total / lower[col][col]
    forward = []
    for row in range(count):
        total = rhs[row]
        for inner in range(row):
            total = total - lower[row][inner] * forward[inner]
        forward.append(total / lower[row][row])
    backward = [None] * count
    for row in reversed(range(count)):
        total = forward[row]
        for inner in range(row + 1, count):
            total = total - lower[inner][row] * backward[inner]
        backward[row] = total / lower[row][row]
    return backward


def newton_step(got, moments, lam, count):
    pairs = pair_list(count)
    norm = got[count]
    first = [got[m] / norm for m in range(count)]
    hess = [[None] * count for _ in range(count)]
    for k, (row, col) in enumerate(pairs):
        second = got[count + 1 + k] / norm
        value = second - first[row] * first[col]
        if row == col:
            value = value + 0.01
        hess[row][col] = value
    rhs = [first[m] - moments[m] for m in range(count)]
    delta = chol_solve(hess, rhs, count)
    return [lam[m] - 0.5 * delta[m] for m in range(count)]


def fit_kernel(t_ref, phit_ref, psi_ref, lam_ref, fit_ref, lam_s, dense_ref):
    spec, levels, cells = t_ref.shape
    count = lam_ref.shape[1]
    used = count + 1 + len(pair_list(count))
    groups = 8 // spec
    part = cells // groups
    highest = lax.Precision.HIGHEST

    def contract(a, b, precision=highest):
        return jnp.dot(a, b, precision=precision, preferred_element_type=jnp.float32)

    def densify(gots):
        for s in range(spec):
            for j in range(groups):
                piece = gots[s][:, j * part : (j + 1) * part]
                row = s * groups + j
                for k in range(used):
                    dense_ref[k, row : row + 1, :] = piece[k : k + 1, :]
        return [dense_ref[k] for k in range(used)]

    def spread(values):
        for m in range(count):
            for s in range(spec):
                for j in range(groups):
                    row = s * groups + j
                    lam_s[s, m : m + 1, j * part : (j + 1) * part] = values[m][row : row + 1, :]

    got = densify([contract(psi_ref[...], t_ref[s]) for s in range(spec)])
    moments = [got[m] / got[count] for m in range(count)]
    lam_s[...] = jnp.zeros(lam_s.shape, jnp.float32)
    zero = jnp.zeros((8, part), jnp.float32)

    def step(_, lam):
        gots = []
        for s in range(spec):
            expo = jnp.exp(contract(phit_ref[...], lam_s[s], LOOP_PRECISION))
            gots.append(contract(psi_ref[...], expo, LOOP_PRECISION))
        new = newton_step(densify(gots), moments, list(lam), count)
        spread(new)
        return tuple(new)

    lax.fori_loop(0, NEWTON, step, tuple([zero] * count))
    for s in range(spec):
        target = t_ref[s]
        exponent = contract(phit_ref[...], lam_s[s])
        log_norm = jnp.log(jnp.sum(jnp.exp(exponent), axis=0, keepdims=True))
        whole = jnp.sum(target, axis=0, keepdims=True)
        ratio = jnp.log(target / whole) - (exponent - log_norm)
        fit_ref[s : s + 1, :] = 2.0 * jnp.sum(target * ratio, axis=0, keepdims=True) / levels
        lam_ref[s] = lam_s[s, 0:count, :]


def legendre_numpy(levels, count):
    xpos = (2.0 * np.arange(levels, dtype=np.float64) + 1.0) / levels - 1.0
    prev = np.ones_like(xpos)
    curr = xpos
    table = [curr]
    for order in range(1, count):
        nxt = ((2 * order + 1) * xpos * curr - order * prev) / (order + 1)
        prev, curr = (curr, nxt)
        table.append(curr)
    return np.stack(table, axis=0).astype(np.float32)


def fit_all(target, count):
    spec, levels, cells = target.shape
    phi = legendre_numpy(levels, count)
    pairs = pair_list(count)
    width = 8
    phit = np.zeros((levels, width), np.float32)
    phit[:, :count] = phi.T
    rows = [phi[m] for m in range(count)] + [np.ones((levels,), np.float32)]
    rows += [phi[r] * phi[c] for r, c in pairs]
    height = -(-len(rows) // 8) * 8
    rows += [np.zeros((levels,), np.float32)] * (height - len(rows))
    psi = np.stack(rows, axis=0)
    return pl.pallas_call(
        fit_kernel,
        out_shape=(
            jax.ShapeDtypeStruct((spec, count, cells), jnp.float32),
            jax.ShapeDtypeStruct((spec, cells), jnp.float32),
        ),
        scratch_shapes=[
            pltpu.VMEM((spec, width, cells), jnp.float32),
            pltpu.VMEM((height, 8, cells * spec // 8), jnp.float32),
        ],
    )(target, jnp.asarray(phit), jnp.asarray(psi))


def smooth_levels(field):
    padded = jnp.pad(field, ((0, 0), (1, 1), (0, 0)))
    return 0.5 * field + 0.25 * (padded[:, :-2, :] + padded[:, 2:, :])


def body_inner(hist, dest, cell_in, offsets):
    rows = hist.shape[0]
    width = hist.shape[2]
    cells = offsets.shape[1]
    devices = lax.axis_size(("cell", "own"))
    capacity = 2 * rows // devices
    slots = devices * capacity
    packed = jnp.sum(hist, axis=1, dtype=jnp.float32).astype(jnp.bfloat16)
    target_block = dest[:, 0]
    member = (target_block[:, None] == jnp.arange(devices, dtype=jnp.int32)[None, :]).astype(
        jnp.int32
    )
    ranks = jnp.sum((jnp.cumsum(member, axis=0) - 1) * member, axis=1)
    position = target_block * capacity + ranks
    codes = jnp.stack([cell_in // CODE + 1, cell_in % CODE], axis=1).astype(jnp.bfloat16)
    codes = jnp.pad(codes, ((0, 0), (0, 128 - 2)))
    payload = jnp.concatenate([packed, codes], axis=1)
    place = (jnp.arange(slots, dtype=jnp.int32)[:, None] == position[None, :]).astype(jnp.bfloat16)
    sent = jnp.dot(place, payload, preferred_element_type=jnp.float32)
    send_rows = sent[:, :width].astype(jnp.bfloat16).reshape(devices, capacity, width)
    code_rows = sent[:, width : width + 2].reshape(devices, capacity, 2)
    code_rows = jnp.swapaxes(code_rows, 1, 2).astype(jnp.bfloat16)
    code_rows = jnp.pad(code_rows, ((0, 0), (0, EXTRA - 2), (0, width - capacity)))
    message = jnp.concatenate([send_rows, code_rows], axis=1)
    got = lax.all_to_all(message, ("cell", "own"), split_axis=0, concat_axis=0, tiled=True)
    lanes = capacity + EXTRA
    recv_rows = got.reshape(devices * lanes, width)
    high = got[:, capacity, :capacity].astype(jnp.int32)
    low = got[:, capacity + 1, :capacity].astype(jnp.int32)
    recv_cells = jnp.where(high > 0, (high - 1) * CODE + low, -1)
    recv_cells = jnp.pad(recv_cells, ((0, 0), (0, EXTRA)), constant_values=-1).reshape(devices * lanes)
    tile = 128
    edges = jnp.concatenate(
        [jnp.arange(tile, dtype=jnp.int32), jnp.arange(cells - tile, cells, dtype=jnp.int32)]
    )
    edge_select = (recv_cells[:, None] == edges[None, :]).astype(jnp.bfloat16)
    edge_sum = lax.dot_general(
        recv_rows, edge_select, (((0,), (0,)), ((), ())), preferred_element_type=jnp.float32
    ).reshape(SPEC, width // SPEC, 2 * tile)
    edge_lev = smooth_levels(edge_sum)
    count = devices
    forward = [(i, i + 1) for i in range(count - 1)]
    backward = [(target, source) for source, target in forward]
    below = lax.ppermute(edge_lev[:, :, 2 * tile - W :], ("cell", "own"), forward)
    above = lax.ppermute(edge_lev[:, :, :W], ("cell", "own"), backward)
    middle = jnp.arange(tile, cells - tile, dtype=jnp.int32)
    select = (recv_cells[:, None] == middle[None, :]).astype(jnp.bfloat16)
    summed = lax.dot_general(
        recv_rows, select, (((0,), (0,)), ((), ())), preferred_element_type=jnp.float32
    )
    cellhist = jnp.concatenate(
        [edge_sum[:, :, :tile], summed.reshape(SPEC, width // SPEC, cells - 2 * tile), edge_sum[:, :, tile:]],
        axis=2,
    )
    levelled = smooth_levels(cellhist)
    rimmed = jnp.concatenate([below, levelled, above], axis=2)
    target = 1.0 + levelled
    for shift in range(-W, W + 1):
        weight = jnp.sum((offsets == shift).astype(jnp.float32), axis=0)
        target = target + weight[None, None, :] * lax.slice_in_dim(
            rimmed, W + shift, W + shift + cells, axis=2
        )
    return fit_all(target, MOM)


def solution(mesh):
    placed = (
        P(("cell", "own"), None, None),
        P(("cell", "own"), None),
        P(("cell", "own")),
        P(None, ("cell", "own")),
    )
    return jax.shard_map(
        body_inner,
        mesh=mesh,
        in_specs=placed,
        out_specs=(P(None, None, ("cell", "own")), P(None, ("cell", "own"))),
        check_vma=False,
    )
```

```python
import jax
import jax.numpy as jnp
import numpy as np
from jax import lax
from jax.experimental import pallas as pl
from jax.experimental.pallas import tpu as pltpu
from jax.sharding import PartitionSpec as P

SPEC = 2
MOM = 6
NEWTON = 8
W = 4
CODE = 32
EXTRA = 8
LOOP_PRECISION = lax.Precision.HIGH


def pair_list(count):
    return [(row, col) for row in range(count) for col in range(row + 1)]


def chol_solve(hess, rhs, count):
    lower = [[None] * count for _ in range(count)]
    for row in range(count):
        for col in range(row + 1):
            total = hess[row][col]
            for inner in range(col):
                total = total - lower[row][inner] * lower[col][inner]
            if row == col:
                lower[row][col] = jnp.sqrt(total)
            else:
                lower[row][col] = total / lower[col][col]
    forward = []
    for row in range(count):
        total = rhs[row]
        for inner in range(row):
            total = total - lower[row][inner] * forward[inner]
        forward.append(total / lower[row][row])
    backward = [None] * count
    for row in reversed(range(count)):
        total = forward[row]
        for inner in range(row + 1, count):
            total = total - lower[inner][row] * backward[inner]
        backward[row] = total / lower[row][row]
    return backward


def newton_step(got, moments, lam, count):
    pairs = pair_list(count)
    norm = got[count]
    first = [got[m] / norm for m in range(count)]
    hess = [[None] * count for _ in range(count)]
    for k, (row, col) in enumerate(pairs):
        second = got[count + 1 + k] / norm
        value = second - first[row] * first[col]
        if row == col:
            value = value + 0.01
        hess[row][col] = value
    rhs = [first[m] - moments[m] for m in range(count)]
    delta = chol_solve(hess, rhs, count)
    return [lam[m] - 0.5 * delta[m] for m in range(count)]


def fit_kernel(t_ref, phit_ref, psi_ref, lam_ref, fit_ref, lam_s, dense_ref):
    spec, levels, cells = t_ref.shape
    count = lam_ref.shape[1]
    used = count + 1 + len(pair_list(count))
    groups = 8 // spec
    part = cells // groups
    highest = lax.Precision.HIGHEST

    def contract(a, b, precision=highest):
        return jnp.dot(a, b, precision=precision, preferred_element_type=jnp.float32)

    def densify(gots):
        for s in range(spec):
            for j in range(groups):
                piece = gots[s][:, j * part : (j + 1) * part]
                row = s * groups + j
                for k in range(used):
                    dense_ref[k, row : row + 1, :] = piece[k : k + 1, :]
        return [dense_ref[k] for k in range(used)]

    def spread(values):
        for m in range(count):
            for s in range(spec):
                for j in range(groups):
                    row = s * groups + j
                    lam_s[s, m : m + 1, j * part : (j + 1) * part] = values[m][row : row + 1, :]

    got = densify([contract(psi_ref[...], t_ref[s]) for s in range(spec)])
    moments = [got[m] / got[count] for m in range(count)]
    lam_s[...] = jnp.zeros(lam_s.shape, jnp.float32)
    zero = jnp.zeros((8, part), jnp.float32)

    def step(_, lam):
        gots = []
        for s in range(spec):
            expo = jnp.exp(contract(phit_ref[...], lam_s[s], LOOP_PRECISION))
            gots.append(contract(psi_ref[...], expo, LOOP_PRECISION))
        new = newton_step(densify(gots), moments, list(lam), count)
        spread(new)
        return tuple(new)

    lax.fori_loop(0, NEWTON, step, tuple([zero] * count))
    for s in range(spec):
        target = t_ref[s]
        exponent = contract(phit_ref[...], lam_s[s])
        log_norm = jnp.log(jnp.sum(jnp.exp(exponent), axis=0, keepdims=True))
        whole = jnp.sum(target, axis=0, keepdims=True)
        ratio = jnp.log(target / whole) - (exponent - log_norm)
        fit_ref[s : s + 1, :] = 2.0 * jnp.sum(target * ratio, axis=0, keepdims=True) / levels
        lam_ref[s] = lam_s[s, 0:count, :]


def legendre_numpy(levels, count):
    xpos = (2.0 * np.arange(levels, dtype=np.float64) + 1.0) / levels - 1.0
    prev = np.ones_like(xpos)
    curr = xpos
    table = [curr]
    for order in range(1, count):
        nxt = ((2 * order + 1) * xpos * curr - order * prev) / (order + 1)
        prev, curr = (curr, nxt)
        table.append(curr)
    return np.stack(table, axis=0).astype(np.float32)


def fit_all(target, count):
    spec, levels, cells = target.shape
    phi = legendre_numpy(levels, count)
    pairs = pair_list(count)
    width = 8
    phit = np.zeros((levels, width), np.float32)
    phit[:, :count] = phi.T
    rows = [phi[m] for m in range(count)] + [np.ones((levels,), np.float32)]
    rows += [phi[r] * phi[c] for r, c in pairs]
    height = -(-len(rows) // 8) * 8
    rows += [np.zeros((levels,), np.float32)] * (height - len(rows))
    psi = np.stack(rows, axis=0)
    return pl.pallas_call(
        fit_kernel,
        out_shape=(
            jax.ShapeDtypeStruct((spec, count, cells), jnp.float32),
            jax.ShapeDtypeStruct((spec, cells), jnp.float32),
        ),
        scratch_shapes=[
            pltpu.VMEM((spec, width, cells), jnp.float32),
            pltpu.VMEM((height, 8, cells * spec // 8), jnp.float32),
        ],
    )(target, jnp.asarray(phit), jnp.asarray(psi))


def smooth_levels(field):
    padded = jnp.pad(field, ((0, 0), (1, 1), (0, 0)))
    return 0.5 * field + 0.25 * (padded[:, :-2, :] + padded[:, 2:, :])


def body_inner(hist, dest, cell_in, offsets):
    rows = hist.shape[0]
    width = hist.shape[2]
    cells = offsets.shape[1]
    devices = lax.axis_size(("cell", "own"))
    capacity = 2 * rows // devices
    slots = devices * capacity
    packed = jnp.sum(hist, axis=1, dtype=jnp.float32).astype(jnp.bfloat16)
    target_block = dest[:, 0]
    member = (target_block[:, None] == jnp.arange(devices, dtype=jnp.int32)[None, :]).astype(
        jnp.int32
    )
    ranks = jnp.sum((jnp.cumsum(member, axis=0) - 1) * member, axis=1)
    position = target_block * capacity + ranks
    place = (jnp.arange(slots, dtype=jnp.int32)[:, None] == position[None, :]).astype(jnp.bfloat16)
    send_rows = jnp.dot(place, packed, preferred_element_type=jnp.float32)
    send_rows = send_rows.astype(jnp.bfloat16).reshape(devices, capacity, width)
    in_rank = (ranks[:, None] == jnp.arange(capacity, dtype=jnp.int32)[None, :]).astype(jnp.bfloat16)
    high_code = (cell_in // CODE + 1).astype(jnp.bfloat16)[:, None] * in_rank
    low_code = (cell_in % CODE).astype(jnp.bfloat16)[:, None] * in_rank
    code_rows = lax.dot_general(
        member.astype(jnp.bfloat16),
        jnp.concatenate([high_code, low_code], axis=1),
        (((0,), (0,)), ((), ())),
        preferred_element_type=jnp.float32,
    )
    code_rows = code_rows.astype(jnp.bfloat16).reshape(devices, 2, capacity)
    code_rows = jnp.pad(code_rows, ((0, 0), (0, EXTRA - 2), (0, width - capacity)))
    message = jnp.concatenate([send_rows, code_rows], axis=1)
    got = lax.all_to_all(message, ("cell", "own"), split_axis=0, concat_axis=0, tiled=True)
    lanes = capacity + EXTRA
    recv_rows = got.reshape(devices * lanes, width)
    high = got[:, capacity, :capacity].astype(jnp.int32)
    low = got[:, capacity + 1, :capacity].astype(jnp.int32)
    recv_cells = jnp.where(high > 0, (high - 1) * CODE + low, -1)
    recv_cells = jnp.pad(recv_cells, ((0, 0), (0, EXTRA)), constant_values=-1).reshape(devices * lanes)
    edges = jnp.concatenate(
        [jnp.arange(W, dtype=jnp.int32), jnp.arange(cells - W, cells, dtype=jnp.int32)]
    )
    edge_select = (recv_cells[:, None] == edges[None, :]).astype(jnp.bfloat16)
    edge_sum = lax.dot_general(
        recv_rows, edge_select, (((0,), (0,)), ((), ())), preferred_element_type=jnp.float32
    )
    edge_lev = smooth_levels(edge_sum.reshape(SPEC, width // SPEC, 2 * W))
    count = devices
    forward = [(i, i + 1) for i in range(count - 1)]
    backward = [(target, source) for source, target in forward]
    below = lax.ppermute(edge_lev[:, :, W:], ("cell", "own"), forward)
    above = lax.ppermute(edge_lev[:, :, :W], ("cell", "own"), backward)
    select = (recv_cells[:, None] == jnp.arange(cells, dtype=jnp.int32)[None, :]).astype(
        jnp.bfloat16
    )
    summed = lax.dot_general(
        recv_rows, select, (((0,), (0,)), ((), ())), preferred_element_type=jnp.float32
    )
    cellhist = summed.reshape(SPEC, width // SPEC, cells)
    levelled = smooth_levels(cellhist)
    rimmed = jnp.concatenate([below, levelled, above], axis=2)
    target = 1.0 + levelled
    for shift in range(-W, W + 1):
        weight = jnp.sum((offsets == shift).astype(jnp.float32), axis=0)
        target = target + weight[None, None, :] * lax.slice_in_dim(
            rimmed, W + shift, W + shift + cells, axis=2
        )
    return fit_all(target, MOM)


def solution(mesh):
    placed = (
        P(("cell", "own"), None, None),
        P(("cell", "own"), None),
        P(("cell", "own")),
        P(None, ("cell", "own")),
    )
    return jax.shard_map(
        body_inner,
        mesh=mesh,
        in_specs=placed,
        out_specs=(P(None, None, ("cell", "own")), P(None, ("cell", "own"))),
        check_vma=False,
    )
```

```python
import jax
import jax.numpy as jnp
import numpy as np
from jax import lax
from jax.experimental import pallas as pl
from jax.experimental.pallas import tpu as pltpu
from jax.sharding import PartitionSpec as P

SPEC = 2
MOM = 6
NEWTON = 8
W = 4
CODE = 32
EXTRA = 8
LOOP_PRECISION = lax.Precision.HIGH


def pair_list(count):
    return [(row, col) for row in range(count) for col in range(row + 1)]


def chol_solve(hess, rhs, count):
    lower = [[None] * count for _ in range(count)]
    for row in range(count):
        for col in range(row + 1):
            total = hess[row][col]
            for inner in range(col):
                total = total - lower[row][inner] * lower[col][inner]
            if row == col:
                lower[row][col] = jnp.sqrt(total)
            else:
                lower[row][col] = total / lower[col][col]
    forward = []
    for row in range(count):
        total = rhs[row]
        for inner in range(row):
            total = total - lower[row][inner] * forward[inner]
        forward.append(total / lower[row][row])
    backward = [None] * count
    for row in reversed(range(count)):
        total = forward[row]
        for inner in range(row + 1, count):
            total = total - lower[inner][row] * backward[inner]
        backward[row] = total / lower[row][row]
    return backward


def newton_step(got, moments, lam, count):
    pairs = pair_list(count)
    norm = got[count]
    first = [got[m] / norm for m in range(count)]
    hess = [[None] * count for _ in range(count)]
    for k, (row, col) in enumerate(pairs):
        second = got[count + 1 + k] / norm
        value = second - first[row] * first[col]
        if row == col:
            value = value + 0.01
        hess[row][col] = value
    rhs = [first[m] - moments[m] for m in range(count)]
    delta = chol_solve(hess, rhs, count)
    return [lam[m] - 0.5 * delta[m] for m in range(count)]


def fit_kernel(t_ref, phit_ref, psi_ref, lam_ref, fit_ref, lam_s, dense_ref):
    spec, levels, cells = t_ref.shape
    count = lam_ref.shape[1]
    used = count + 1 + len(pair_list(count))
    groups = 8 // spec
    part = cells // groups
    highest = lax.Precision.HIGHEST

    def contract(a, b, precision=highest):
        return jnp.dot(a, b, precision=precision, preferred_element_type=jnp.float32)

    def densify(gots):
        for s in range(spec):
            for j in range(groups):
                piece = gots[s][:, j * part : (j + 1) * part]
                row = s * groups + j
                for k in range(used):
                    dense_ref[k, row : row + 1, :] = piece[k : k + 1, :]
        return [dense_ref[k] for k in range(used)]

    def spread(values):
        for m in range(count):
            for s in range(spec):
                for j in range(groups):
                    row = s * groups + j
                    lam_s[s, m : m + 1, j * part : (j + 1) * part] = values[m][row : row + 1, :]

    got = densify([contract(psi_ref[...], t_ref[s]) for s in range(spec)])
    moments = [got[m] / got[count] for m in range(count)]
    lam_s[...] = jnp.zeros(lam_s.shape, jnp.float32)
    zero = jnp.zeros((8, part), jnp.float32)

    def step(_, lam):
        gots = []
        for s in range(spec):
            expo = jnp.exp(contract(phit_ref[...], lam_s[s], LOOP_PRECISION))
            gots.append(contract(psi_ref[...], expo, LOOP_PRECISION))
        new = newton_step(densify(gots), moments, list(lam), count)
        spread(new)
        return tuple(new)

    lax.fori_loop(0, NEWTON, step, tuple([zero] * count))
    for s in range(spec):
        target = t_ref[s]
        exponent = contract(phit_ref[...], lam_s[s])
        log_norm = jnp.log(jnp.sum(jnp.exp(exponent), axis=0, keepdims=True))
        whole = jnp.sum(target, axis=0, keepdims=True)
        ratio = jnp.log(target / whole) - (exponent - log_norm)
        fit_ref[s : s + 1, :] = 2.0 * jnp.sum(target * ratio, axis=0, keepdims=True) / levels
        lam_ref[s] = lam_s[s, 0:count, :]


def legendre_numpy(levels, count):
    xpos = (2.0 * np.arange(levels, dtype=np.float64) + 1.0) / levels - 1.0
    prev = np.ones_like(xpos)
    curr = xpos
    table = [curr]
    for order in range(1, count):
        nxt = ((2 * order + 1) * xpos * curr - order * prev) / (order + 1)
        prev, curr = (curr, nxt)
        table.append(curr)
    return np.stack(table, axis=0).astype(np.float32)


def fit_all(target, count):
    spec, levels, cells = target.shape
    phi = legendre_numpy(levels, count)
    pairs = pair_list(count)
    width = 8
    phit = np.zeros((levels, width), np.float32)
    phit[:, :count] = phi.T
    rows = [phi[m] for m in range(count)] + [np.ones((levels,), np.float32)]
    rows += [phi[r] * phi[c] for r, c in pairs]
    height = -(-len(rows) // 8) * 8
    rows += [np.zeros((levels,), np.float32)] * (height - len(rows))
    psi = np.stack(rows, axis=0)
    return pl.pallas_call(
        fit_kernel,
        out_shape=(
            jax.ShapeDtypeStruct((spec, count, cells), jnp.float32),
            jax.ShapeDtypeStruct((spec, cells), jnp.float32),
        ),
        scratch_shapes=[
            pltpu.VMEM((spec, width, cells), jnp.float32),
            pltpu.VMEM((height, 8, cells * spec // 8), jnp.float32),
        ],
    )(target, jnp.asarray(phit), jnp.asarray(psi))


def smooth_levels(field):
    padded = jnp.pad(field, ((0, 0), (1, 1), (0, 0)))
    return 0.5 * field + 0.25 * (padded[:, :-2, :] + padded[:, 2:, :])


def body_inner(hist, dest, cell_in, offsets):
    rows = hist.shape[0]
    width = hist.shape[2]
    cells = offsets.shape[1]
    devices = lax.axis_size(("cell", "own"))
    capacity = 2 * rows // devices
    slots = devices * capacity
    packed = jnp.sum(hist, axis=1, dtype=jnp.float32).astype(jnp.bfloat16)
    target_block = dest[:, 0]
    member = (target_block[:, None] == jnp.arange(devices, dtype=jnp.int32)[None, :]).astype(
        jnp.int32
    )
    ranks = jnp.sum((jnp.cumsum(member, axis=0) - 1) * member, axis=1)
    position = target_block * capacity + ranks
    codes = jnp.stack([cell_in // CODE + 1, cell_in % CODE], axis=1).astype(jnp.bfloat16)
    codes = jnp.pad(codes, ((0, 0), (0, 128 - 2)))
    payload = jnp.concatenate([packed, codes], axis=1)
    place = (jnp.arange(slots, dtype=jnp.int32)[:, None] == position[None, :]).astype(jnp.bfloat16)
    sent = jnp.dot(place, payload, preferred_element_type=jnp.float32)
    send_rows = sent[:, :width].astype(jnp.bfloat16).reshape(devices, capacity, width)
    code_rows = sent[:, width : width + 2].reshape(devices, capacity, 2)
    code_rows = jnp.swapaxes(code_rows, 1, 2).astype(jnp.bfloat16)
    code_rows = jnp.pad(code_rows, ((0, 0), (0, EXTRA - 2), (0, width - capacity)))
    message = jnp.concatenate([send_rows, code_rows], axis=1)
    low_side = cell_in < W
    high_side = cell_in >= cells - W
    aimed = jnp.where(high_side, target_block + 1, target_block - 1)
    aimed_ok = (low_side | high_side) & (aimed >= 0) & (aimed < devices)
    spot = jnp.where(high_side, cell_in - (cells - W), W + cell_in)
    halo_slot = jnp.where(aimed_ok, aimed * 2 * W + spot, -1)
    halo_place = (
        jnp.arange(devices * 2 * W, dtype=jnp.int32)[:, None] == halo_slot[None, :]
    ).astype(jnp.bfloat16)
    halo_part = jnp.dot(halo_place, packed, preferred_element_type=jnp.float32)
    halo_sum = lax.psum_scatter(
        halo_part.reshape(devices, 2 * W, width), ("cell", "own"), scatter_dimension=0, tiled=True
    )
    got = lax.all_to_all(message, ("cell", "own"), split_axis=0, concat_axis=0, tiled=True)
    lanes = capacity + EXTRA
    recv_rows = got.reshape(devices * lanes, width)
    high = got[:, capacity, :capacity].astype(jnp.int32)
    low = got[:, capacity + 1, :capacity].astype(jnp.int32)
    recv_cells = jnp.where(high > 0, (high - 1) * CODE + low, -1)
    recv_cells = jnp.pad(recv_cells, ((0, 0), (0, EXTRA)), constant_values=-1).reshape(devices * lanes)
    halo_lev = smooth_levels(halo_sum.reshape(2 * W, width).T.reshape(SPEC, width // SPEC, 2 * W))
    below = halo_lev[:, :, :W]
    above = halo_lev[:, :, W:]
    select = (recv_cells[:, None] == jnp.arange(cells, dtype=jnp.int32)[None, :]).astype(
        jnp.bfloat16
    )
    summed = lax.dot_general(
        recv_rows, select, (((0,), (0,)), ((), ())), preferred_element_type=jnp.float32
    )
    cellhist = summed.reshape(SPEC, width // SPEC, cells)
    levelled = smooth_levels(cellhist)
    rimmed = jnp.concatenate([below, levelled, above], axis=2)
    target = 1.0 + levelled
    for shift in range(-W, W + 1):
        weight = jnp.sum((offsets == shift).astype(jnp.float32), axis=0)
        target = target + weight[None, None, :] * lax.slice_in_dim(
            rimmed, W + shift, W + shift + cells, axis=2
        )
    return fit_all(target, MOM)


def solution(mesh):
    placed = (
        P(("cell", "own"), None, None),
        P(("cell", "own"), None),
        P(("cell", "own")),
        P(None, ("cell", "own")),
    )
    return jax.shard_map(
        body_inner,
        mesh=mesh,
        in_specs=placed,
        out_specs=(P(None, None, ("cell", "own")), P(None, ("cell", "own"))),
        check_vma=False,
    )
```

```python
import jax
import jax.numpy as jnp
import numpy as np
from jax import lax
from jax.experimental import pallas as pl
from jax.experimental.pallas import tpu as pltpu
from jax.sharding import PartitionSpec as P

SPEC = 2
MOM = 6
NEWTON = 8
W = 4
CODE = 32
EXTRA = 8
LOOP_PRECISION = lax.Precision.HIGH


def pair_list(count):
    return [(row, col) for row in range(count) for col in range(row + 1)]


def chol_solve(hess, rhs, count):
    lower = [[None] * count for _ in range(count)]
    for row in range(count):
        for col in range(row + 1):
            total = hess[row][col]
            for inner in range(col):
                total = total - lower[row][inner] * lower[col][inner]
            if row == col:
                lower[row][col] = jnp.sqrt(total)
            else:
                lower[row][col] = total / lower[col][col]
    forward = []
    for row in range(count):
        total = rhs[row]
        for inner in range(row):
            total = total - lower[row][inner] * forward[inner]
        forward.append(total / lower[row][row])
    backward = [None] * count
    for row in reversed(range(count)):
        total = forward[row]
        for inner in range(row + 1, count):
            total = total - lower[inner][row] * backward[inner]
        backward[row] = total / lower[row][row]
    return backward


def newton_step(got, moments, lam, count):
    pairs = pair_list(count)
    norm = got[count]
    first = [got[m] / norm for m in range(count)]
    hess = [[None] * count for _ in range(count)]
    for k, (row, col) in enumerate(pairs):
        second = got[count + 1 + k] / norm
        value = second - first[row] * first[col]
        if row == col:
            value = value + 0.01
        hess[row][col] = value
    rhs = [first[m] - moments[m] for m in range(count)]
    delta = chol_solve(hess, rhs, count)
    return [lam[m] - 0.5 * delta[m] for m in range(count)]


def fit_kernel(t_ref, phit_ref, psi_ref, lam_ref, fit_ref, lam_s, dense_ref):
    spec, levels, cells = t_ref.shape
    count = lam_ref.shape[1]
    used = count + 1 + len(pair_list(count))
    groups = 8 // spec
    part = cells // groups
    highest = lax.Precision.HIGHEST

    def contract(a, b, precision=highest):
        return jnp.dot(a, b, precision=precision, preferred_element_type=jnp.float32)

    def densify(gots):
        for s in range(spec):
            for j in range(groups):
                piece = gots[s][:, j * part : (j + 1) * part]
                row = s * groups + j
                for k in range(used):
                    dense_ref[k, row : row + 1, :] = piece[k : k + 1, :]
        return [dense_ref[k] for k in range(used)]

    def spread(values):
        for m in range(count):
            for s in range(spec):
                for j in range(groups):
                    row = s * groups + j
                    lam_s[s, m : m + 1, j * part : (j + 1) * part] = values[m][row : row + 1, :]

    got = densify([contract(psi_ref[...], t_ref[s]) for s in range(spec)])
    moments = [got[m] / got[count] for m in range(count)]
    lam_s[...] = jnp.zeros(lam_s.shape, jnp.float32)
    zero = jnp.zeros((8, part), jnp.float32)

    def step(_, lam):
        gots = []
        for s in range(spec):
            expo = jnp.exp(contract(phit_ref[...], lam_s[s], LOOP_PRECISION))
            gots.append(contract(psi_ref[...], expo, LOOP_PRECISION))
        new = newton_step(densify(gots), moments, list(lam), count)
        spread(new)
        return tuple(new)

    lax.fori_loop(0, NEWTON, step, tuple([zero] * count))
    for s in range(spec):
        target = t_ref[s]
        exponent = contract(phit_ref[...], lam_s[s])
        log_norm = jnp.log(jnp.sum(jnp.exp(exponent), axis=0, keepdims=True))
        whole = jnp.sum(target, axis=0, keepdims=True)
        ratio = jnp.log(target / whole) - (exponent - log_norm)
        fit_ref[s : s + 1, :] = 2.0 * jnp.sum(target * ratio, axis=0, keepdims=True) / levels
        lam_ref[s] = lam_s[s, 0:count, :]


def legendre_numpy(levels, count):
    xpos = (2.0 * np.arange(levels, dtype=np.float64) + 1.0) / levels - 1.0
    prev = np.ones_like(xpos)
    curr = xpos
    table = [curr]
    for order in range(1, count):
        nxt = ((2 * order + 1) * xpos * curr - order * prev) / (order + 1)
        prev, curr = (curr, nxt)
        table.append(curr)
    return np.stack(table, axis=0).astype(np.float32)


def fit_all(target, count):
    spec, levels, cells = target.shape
    phi = legendre_numpy(levels, count)
    pairs = pair_list(count)
    width = 8
    phit = np.zeros((levels, width), np.float32)
    phit[:, :count] = phi.T
    rows = [phi[m] for m in range(count)] + [np.ones((levels,), np.float32)]
    rows += [phi[r] * phi[c] for r, c in pairs]
    height = -(-len(rows) // 8) * 8
    rows += [np.zeros((levels,), np.float32)] * (height - len(rows))
    psi = np.stack(rows, axis=0)
    return pl.pallas_call(
        fit_kernel,
        out_shape=(
            jax.ShapeDtypeStruct((spec, count, cells), jnp.float32),
            jax.ShapeDtypeStruct((spec, cells), jnp.float32),
        ),
        scratch_shapes=[
            pltpu.VMEM((spec, width, cells), jnp.float32),
            pltpu.VMEM((height, 8, cells * spec // 8), jnp.float32),
        ],
    )(target, jnp.asarray(phit), jnp.asarray(psi))


def smooth_levels(field):
    padded = jnp.pad(field, ((0, 0), (1, 1), (0, 0)))
    return 0.5 * field + 0.25 * (padded[:, :-2, :] + padded[:, 2:, :])


def body_inner(hist, dest, cell_in, offsets):
    rows = hist.shape[0]
    width = hist.shape[2]
    cells = offsets.shape[1]
    devices = lax.axis_size(("cell", "own"))
    capacity = 2 * rows // devices
    slots = devices * capacity
    packed = jnp.sum(hist, axis=1, dtype=jnp.float32).astype(jnp.bfloat16)
    target_block = dest[:, 0]
    member = (target_block[:, None] == jnp.arange(devices, dtype=jnp.int32)[None, :]).astype(
        jnp.int32
    )
    ranks = jnp.sum((jnp.cumsum(member, axis=0) - 1) * member, axis=1)
    position = target_block * capacity + ranks
    codes = jnp.stack([cell_in // CODE + 1, cell_in % CODE], axis=1).astype(jnp.bfloat16)
    codes = jnp.pad(codes, ((0, 0), (0, 128 - 2)))
    payload = jnp.concatenate([packed, codes], axis=1)
    place = (jnp.arange(slots, dtype=jnp.int32)[:, None] == position[None, :]).astype(jnp.bfloat16)
    sent = jnp.dot(place, payload, preferred_element_type=jnp.float32)
    send_rows = sent[:, :width].astype(jnp.bfloat16).reshape(devices, capacity, width)
    code_rows = sent[:, width : width + 2].reshape(devices, capacity, 2)
    code_rows = jnp.swapaxes(code_rows, 1, 2).astype(jnp.bfloat16)
    code_rows = jnp.pad(code_rows, ((0, 0), (0, EXTRA - 2), (0, width - capacity)))
    message = jnp.concatenate([send_rows, code_rows], axis=1)
    got = lax.all_to_all(message, ("cell", "own"), split_axis=0, concat_axis=0, tiled=True)
    lanes = capacity + EXTRA
    recv_rows = got.reshape(devices * lanes, width)
    high = got[:, capacity, :capacity].astype(jnp.int32)
    low = got[:, capacity + 1, :capacity].astype(jnp.int32)
    recv_cells = jnp.where(high > 0, (high - 1) * CODE + low, -1)
    recv_cells = jnp.pad(recv_cells, ((0, 0), (0, EXTRA)), constant_values=-1).reshape(devices * lanes)
    tile = 128

    def cell_sums(first, count):
        picked = (
            recv_cells[:, None] == first + jnp.arange(count, dtype=jnp.int32)[None, :]
        ).astype(jnp.bfloat16)
        summed = lax.dot_general(
            recv_rows, picked, (((0,), (0,)), ((), ())), preferred_element_type=jnp.float32
        )
        return summed.reshape(SPEC, width // SPEC, count)

    bottom = cell_sums(0, tile)
    top = cell_sums(cells - tile, tile)
    forward = [(i, i + 1) for i in range(devices - 1)]
    backward = [(target, source) for source, target in forward]
    below = lax.ppermute(smooth_levels(top)[:, :, tile - W :], ("cell", "own"), forward)
    above = lax.ppermute(smooth_levels(bottom)[:, :, :W], ("cell", "own"), backward)
    middle = cell_sums(tile, cells - 2 * tile)
    cellhist = jnp.concatenate([bottom, middle, top], axis=2)
    levelled = smooth_levels(cellhist)
    rimmed = jnp.concatenate([below, levelled, above], axis=2)
    target = 1.0 + levelled
    for shift in range(-W, W + 1):
        weight = jnp.sum((offsets == shift).astype(jnp.float32), axis=0)
        target = target + weight[None, None, :] * lax.slice_in_dim(
            rimmed, W + shift, W + shift + cells, axis=2
        )
    return fit_all(target, MOM)


def solution(mesh):
    placed = (
        P(("cell", "own"), None, None),
        P(("cell", "own"), None),
        P(("cell", "own")),
        P(None, ("cell", "own")),
    )
    return jax.shard_map(
        body_inner,
        mesh=mesh,
        in_specs=placed,
        out_specs=(P(None, None, ("cell", "own")), P(None, ("cell", "own"))),
        check_vma=False,
    )
```

```python
import jax
import jax.numpy as jnp
import numpy as np
from jax import lax
from jax.experimental import pallas as pl
from jax.experimental.pallas import tpu as pltpu
from jax.sharding import PartitionSpec as P

SPEC = 2
MOM = 6
NEWTON = 8
W = 4
CODE = 32
EXTRA = 8
LOOP_PRECISION = lax.Precision.HIGH


def pair_list(count):
    return [(row, col) for row in range(count) for col in range(row + 1)]


def chol_solve(hess, rhs, count):
    lower = [[None] * count for _ in range(count)]
    for row in range(count):
        for col in range(row + 1):
            total = hess[row][col]
            for inner in range(col):
                total = total - lower[row][inner] * lower[col][inner]
            if row == col:
                lower[row][col] = jnp.sqrt(total)
            else:
                lower[row][col] = total / lower[col][col]
    forward = []
    for row in range(count):
        total = rhs[row]
        for inner in range(row):
            total = total - lower[row][inner] * forward[inner]
        forward.append(total / lower[row][row])
    backward = [None] * count
    for row in reversed(range(count)):
        total = forward[row]
        for inner in range(row + 1, count):
            total = total - lower[inner][row] * backward[inner]
        backward[row] = total / lower[row][row]
    return backward


def newton_step(got, moments, lam, count):
    pairs = pair_list(count)
    norm = got[count]
    first = [got[m] / norm for m in range(count)]
    hess = [[None] * count for _ in range(count)]
    for k, (row, col) in enumerate(pairs):
        second = got[count + 1 + k] / norm
        value = second - first[row] * first[col]
        if row == col:
            value = value + 0.01
        hess[row][col] = value
    rhs = [first[m] - moments[m] for m in range(count)]
    delta = chol_solve(hess, rhs, count)
    return [lam[m] - 0.5 * delta[m] for m in range(count)]


def fit_kernel(t_ref, phit_ref, psi_ref, lam_ref, fit_ref, lam_s, dense_ref):
    spec, levels, cells = t_ref.shape
    count = lam_ref.shape[0]
    used = count + 1 + len(pair_list(count))
    groups = 8 // spec
    part = cells // groups
    highest = lax.Precision.HIGHEST

    def contract(a, b, precision=highest):
        return jnp.dot(a, b, precision=precision, preferred_element_type=jnp.float32)

    def densify(gots):
        for s in range(spec):
            for j in range(groups):
                piece = gots[s][:, j * part : (j + 1) * part]
                row = s * groups + j
                for k in range(used):
                    dense_ref[k, row : row + 1, :] = piece[k : k + 1, :]
        return [dense_ref[k] for k in range(used)]

    def spread(values):
        for m in range(count):
            for s in range(spec):
                for j in range(groups):
                    row = s * groups + j
                    lam_s[s, m : m + 1, j * part : (j + 1) * part] = values[m][row : row + 1, :]

    got = densify([contract(psi_ref[...], t_ref[s]) for s in range(spec)])
    moments = [got[m] / got[count] for m in range(count)]
    lam_s[...] = jnp.zeros(lam_s.shape, jnp.float32)
    zero = jnp.zeros((8, part), jnp.float32)

    def step(_, lam):
        gots = []
        for s in range(spec):
            expo = jnp.exp(contract(phit_ref[...], lam_s[s], LOOP_PRECISION))
            gots.append(contract(psi_ref[...], expo, LOOP_PRECISION))
        new = newton_step(densify(gots), moments, list(lam), count)
        spread(new)
        return tuple(new)

    lax.fori_loop(0, NEWTON, step, tuple([zero] * count))
    for s in range(spec):
        target = t_ref[s]
        exponent = contract(phit_ref[...], lam_s[s])
        log_norm = jnp.log(jnp.sum(jnp.exp(exponent), axis=0, keepdims=True))
        whole = jnp.sum(target, axis=0, keepdims=True)
        ratio = jnp.log(target / whole) - (exponent - log_norm)
        fit_ref[s : s + 1, :] = 2.0 * jnp.sum(target * ratio, axis=0, keepdims=True) / levels
        for m in range(count):
            lam_ref[m, s : s + 1, :] = lam_s[s, m : m + 1, :]


def legendre_numpy(levels, count):
    xpos = (2.0 * np.arange(levels, dtype=np.float64) + 1.0) / levels - 1.0
    prev = np.ones_like(xpos)
    curr = xpos
    table = [curr]
    for order in range(1, count):
        nxt = ((2 * order + 1) * xpos * curr - order * prev) / (order + 1)
        prev, curr = (curr, nxt)
        table.append(curr)
    return np.stack(table, axis=0).astype(np.float32)


def fit_all(target, count):
    spec, levels, cells = target.shape
    phi = legendre_numpy(levels, count)
    pairs = pair_list(count)
    width = 8
    phit = np.zeros((levels, width), np.float32)
    phit[:, :count] = phi.T
    rows = [phi[m] for m in range(count)] + [np.ones((levels,), np.float32)]
    rows += [phi[r] * phi[c] for r, c in pairs]
    height = -(-len(rows) // 8) * 8
    rows += [np.zeros((levels,), np.float32)] * (height - len(rows))
    psi = np.stack(rows, axis=0)
    lam, fit = pl.pallas_call(
        fit_kernel,
        out_shape=(
            jax.ShapeDtypeStruct((count, spec, cells), jnp.float32),
            jax.ShapeDtypeStruct((spec, cells), jnp.float32),
        ),
        scratch_shapes=[
            pltpu.VMEM((spec, width, cells), jnp.float32),
            pltpu.VMEM((height, 8, cells * spec // 8), jnp.float32),
        ],
    )(target, jnp.asarray(phit), jnp.asarray(psi))
    return jnp.transpose(lam, (1, 0, 2)), fit


def smooth_levels(field):
    padded = jnp.pad(field, ((0, 0), (1, 1), (0, 0)))
    return 0.5 * field + 0.25 * (padded[:, :-2, :] + padded[:, 2:, :])


def body_inner(hist, dest, cell_in, offsets):
    rows = hist.shape[0]
    width = hist.shape[2]
    cells = offsets.shape[1]
    devices = lax.axis_size(("cell", "own"))
    capacity = 2 * rows // devices
    slots = devices * capacity
    packed = jnp.sum(hist, axis=1, dtype=jnp.float32).astype(jnp.bfloat16)
    target_block = dest[:, 0]
    member = (target_block[:, None] == jnp.arange(devices, dtype=jnp.int32)[None, :]).astype(
        jnp.int32
    )
    ranks = jnp.sum((jnp.cumsum(member, axis=0) - 1) * member, axis=1)
    position = target_block * capacity + ranks
    codes = jnp.stack([cell_in // CODE + 1, cell_in % CODE], axis=1).astype(jnp.bfloat16)
    codes = jnp.pad(codes, ((0, 0), (0, 128 - 2)))
    payload = jnp.concatenate([packed, codes], axis=1)
    place = (jnp.arange(slots, dtype=jnp.int32)[:, None] == position[None, :]).astype(jnp.bfloat16)
    sent = jnp.dot(place, payload, preferred_element_type=jnp.float32)
    send_rows = sent[:, :width].astype(jnp.bfloat16).reshape(devices, capacity, width)
    code_rows = sent[:, width : width + 2].reshape(devices, capacity, 2)
    code_rows = jnp.swapaxes(code_rows, 1, 2).astype(jnp.bfloat16)
    code_rows = jnp.pad(code_rows, ((0, 0), (0, EXTRA - 2), (0, width - capacity)))
    message = jnp.concatenate([send_rows, code_rows], axis=1)
    got = lax.all_to_all(message, ("cell", "own"), split_axis=0, concat_axis=0, tiled=True)
    lanes = capacity + EXTRA
    recv_rows = got.reshape(devices * lanes, width)
    high = got[:, capacity, :capacity].astype(jnp.int32)
    low = got[:, capacity + 1, :capacity].astype(jnp.int32)
    recv_cells = jnp.where(high > 0, (high - 1) * CODE + low, -1)
    recv_cells = jnp.pad(recv_cells, ((0, 0), (0, EXTRA)), constant_values=-1).reshape(devices * lanes)
    edges = jnp.concatenate(
        [jnp.arange(W, dtype=jnp.int32), jnp.arange(cells - W, cells, dtype=jnp.int32)]
    )
    edge_select = (recv_cells[:, None] == edges[None, :]).astype(jnp.bfloat16)
    edge_sum = lax.dot_general(
        recv_rows, edge_select, (((0,), (0,)), ((), ())), preferred_element_type=jnp.float32
    )
    edge_lev = smooth_levels(edge_sum.reshape(SPEC, width // SPEC, 2 * W))
    count = devices
    forward = [(i, i + 1) for i in range(count - 1)]
    backward = [(target, source) for source, target in forward]
    below = lax.ppermute(edge_lev[:, :, W:], ("cell", "own"), forward)
    above = lax.ppermute(edge_lev[:, :, :W], ("cell", "own"), backward)
    select = (recv_cells[:, None] == jnp.arange(cells, dtype=jnp.int32)[None, :]).astype(
        jnp.bfloat16
    )
    summed = lax.dot_general(
        recv_rows, select, (((0,), (0,)), ((), ())), preferred_element_type=jnp.float32
    )
    cellhist = summed.reshape(SPEC, width // SPEC, cells)
    levelled = smooth_levels(cellhist)
    rimmed = jnp.concatenate([below, levelled, above], axis=2)
    target = 1.0 + levelled
    for shift in range(-W, W + 1):
        weight = jnp.sum((offsets == shift).astype(jnp.float32), axis=0)
        target = target + weight[None, None, :] * lax.slice_in_dim(
            rimmed, W + shift, W + shift + cells, axis=2
        )
    return fit_all(target, MOM)


def solution(mesh):
    placed = (
        P(("cell", "own"), None, None),
        P(("cell", "own"), None),
        P(("cell", "own")),
        P(None, ("cell", "own")),
    )
    return jax.shard_map(
        body_inner,
        mesh=mesh,
        in_specs=placed,
        out_specs=(P(None, None, ("cell", "own")), P(None, ("cell", "own"))),
        check_vma=False,
    )
```

```python
import jax
import jax.numpy as jnp
import numpy as np
from jax import lax
from jax.experimental import pallas as pl
from jax.experimental.pallas import tpu as pltpu
from jax.sharding import PartitionSpec as P

SPEC = 2
MOM = 6
NEWTON = 8
W = 4
CODE = 32
EXTRA = 8
LOOP_PRECISION = lax.Precision.HIGH


def pair_list(count):
    return [(row, col) for row in range(count) for col in range(row + 1)]


def chol_solve(hess, rhs, count):
    lower = [[None] * count for _ in range(count)]
    for row in range(count):
        for col in range(row + 1):
            total = hess[row][col]
            for inner in range(col):
                total = total - lower[row][inner] * lower[col][inner]
            if row == col:
                lower[row][col] = jnp.sqrt(total)
            else:
                lower[row][col] = total / lower[col][col]
    forward = []
    for row in range(count):
        total = rhs[row]
        for inner in range(row):
            total = total - lower[row][inner] * forward[inner]
        forward.append(total / lower[row][row])
    backward = [None] * count
    for row in reversed(range(count)):
        total = forward[row]
        for inner in range(row + 1, count):
            total = total - lower[inner][row] * backward[inner]
        backward[row] = total / lower[row][row]
    return backward


def newton_step(got, moments, lam, count):
    pairs = pair_list(count)
    norm = got[count]
    first = [got[m] / norm for m in range(count)]
    hess = [[None] * count for _ in range(count)]
    for k, (row, col) in enumerate(pairs):
        second = got[count + 1 + k] / norm
        value = second - first[row] * first[col]
        if row == col:
            value = value + 0.01
        hess[row][col] = value
    rhs = [first[m] - moments[m] for m in range(count)]
    delta = chol_solve(hess, rhs, count)
    return [lam[m] - 0.5 * delta[m] for m in range(count)]


def fit_kernel(
    h_ref, rim_ref, w_ref, phit_ref, psi_ref, lam_ref, fit_ref, lam_s, dense_ref, t_ref, ext_ref
):
    spec, levels, cells = h_ref.shape
    pad = (ext_ref.shape[2] - cells) // 2
    rim = rim_ref.shape[2] // 2
    ext_ref[...] = jnp.zeros(ext_ref.shape, jnp.float32)
    for s in range(spec):
        field = h_ref[s]
        t_ref[s] = field
        lower = jnp.concatenate([jnp.zeros((1, cells), jnp.float32), t_ref[s, : levels - 1, :]], axis=0)
        upper = jnp.concatenate([t_ref[s, 1:, :], jnp.zeros((1, cells), jnp.float32)], axis=0)
        levelled = 0.5 * field + 0.25 * (lower + upper)
        ext_ref[s, :, pad : pad + cells] = levelled
        ext_ref[s, :, pad - rim : pad] = rim_ref[s, :, :rim]
        ext_ref[s, :, pad + cells : pad + cells + rim] = rim_ref[s, :, rim:]
        target = 1.0 + levelled
        for k in range(w_ref.shape[0]):
            shift = k - w_ref.shape[0] // 2
            target = target + w_ref[k : k + 1, :] * ext_ref[s, :, pad + shift : pad + shift + cells]
        t_ref[s] = target
    count = lam_ref.shape[0]
    used = count + 1 + len(pair_list(count))
    groups = 8 // spec
    part = cells // groups
    highest = lax.Precision.HIGHEST

    def contract(a, b, precision=highest):
        return jnp.dot(a, b, precision=precision, preferred_element_type=jnp.float32)

    def densify(gots):
        for s in range(spec):
            for j in range(groups):
                piece = gots[s][:, j * part : (j + 1) * part]
                row = s * groups + j
                for k in range(used):
                    dense_ref[k, row : row + 1, :] = piece[k : k + 1, :]
        return [dense_ref[k] for k in range(used)]

    def spread(values):
        for m in range(count):
            for s in range(spec):
                for j in range(groups):
                    row = s * groups + j
                    lam_s[s, m : m + 1, j * part : (j + 1) * part] = values[m][row : row + 1, :]

    got = densify([contract(psi_ref[...], t_ref[s]) for s in range(spec)])
    moments = [got[m] / got[count] for m in range(count)]
    lam_s[...] = jnp.zeros(lam_s.shape, jnp.float32)
    zero = jnp.zeros((8, part), jnp.float32)

    def step(_, lam):
        gots = []
        for s in range(spec):
            expo = jnp.exp(contract(phit_ref[...], lam_s[s], LOOP_PRECISION))
            gots.append(contract(psi_ref[...], expo, LOOP_PRECISION))
        new = newton_step(densify(gots), moments, list(lam), count)
        spread(new)
        return tuple(new)

    lax.fori_loop(0, NEWTON, step, tuple([zero] * count))
    for s in range(spec):
        target = t_ref[s]
        exponent = contract(phit_ref[...], lam_s[s])
        log_norm = jnp.log(jnp.sum(jnp.exp(exponent), axis=0, keepdims=True))
        whole = jnp.sum(target, axis=0, keepdims=True)
        ratio = jnp.log(target / whole) - (exponent - log_norm)
        fit_ref[s : s + 1, :] = 2.0 * jnp.sum(target * ratio, axis=0, keepdims=True) / levels
        for m in range(count):
            lam_ref[m, s : s + 1, :] = lam_s[s, m : m + 1, :]


def legendre_numpy(levels, count):
    xpos = (2.0 * np.arange(levels, dtype=np.float64) + 1.0) / levels - 1.0
    prev = np.ones_like(xpos)
    curr = xpos
    table = [curr]
    for order in range(1, count):
        nxt = ((2 * order + 1) * xpos * curr - order * prev) / (order + 1)
        prev, curr = (curr, nxt)
        table.append(curr)
    return np.stack(table, axis=0).astype(np.float32)


def fit_all(cellhist, rim, weights, count):
    spec, levels, cells = cellhist.shape
    phi = legendre_numpy(levels, count)
    pairs = pair_list(count)
    width = 8
    phit = np.zeros((levels, width), np.float32)
    phit[:, :count] = phi.T
    rows = [phi[m] for m in range(count)] + [np.ones((levels,), np.float32)]
    rows += [phi[r] * phi[c] for r, c in pairs]
    height = -(-len(rows) // 8) * 8
    rows += [np.zeros((levels,), np.float32)] * (height - len(rows))
    psi = np.stack(rows, axis=0)
    lam, fit = pl.pallas_call(
        fit_kernel,
        out_shape=(
            jax.ShapeDtypeStruct((count, spec, cells), jnp.float32),
            jax.ShapeDtypeStruct((spec, cells), jnp.float32),
        ),
        scratch_shapes=[
            pltpu.VMEM((spec, width, cells), jnp.float32),
            pltpu.VMEM((height, 8, cells * spec // 8), jnp.float32),
            pltpu.VMEM((spec, levels, cells), jnp.float32),
            pltpu.VMEM((spec, levels, cells + 256), jnp.float32),
        ],
    )(cellhist, rim, weights, jnp.asarray(phit), jnp.asarray(psi))
    return jnp.transpose(lam, (1, 0, 2)), fit


def smooth_levels(field):
    padded = jnp.pad(field, ((0, 0), (1, 1), (0, 0)))
    return 0.5 * field + 0.25 * (padded[:, :-2, :] + padded[:, 2:, :])


def body_inner(hist, dest, cell_in, offsets):
    rows = hist.shape[0]
    width = hist.shape[2]
    cells = offsets.shape[1]
    devices = lax.axis_size(("cell", "own"))
    capacity = 2 * rows // devices
    slots = devices * capacity
    packed = jnp.sum(hist, axis=1, dtype=jnp.float32).astype(jnp.bfloat16)
    target_block = dest[:, 0]
    member = (target_block[:, None] == jnp.arange(devices, dtype=jnp.int32)[None, :]).astype(
        jnp.int32
    )
    ranks = jnp.sum((jnp.cumsum(member, axis=0) - 1) * member, axis=1)
    position = target_block * capacity + ranks
    codes = jnp.stack([cell_in // CODE + 1, cell_in % CODE], axis=1).astype(jnp.bfloat16)
    codes = jnp.pad(codes, ((0, 0), (0, 128 - 2)))
    payload = jnp.concatenate([packed, codes], axis=1)
    place = (jnp.arange(slots, dtype=jnp.int32)[:, None] == position[None, :]).astype(jnp.bfloat16)
    sent = jnp.dot(place, payload, preferred_element_type=jnp.float32)
    send_rows = sent[:, :width].astype(jnp.bfloat16).reshape(devices, capacity, width)
    code_rows = sent[:, width : width + 2].reshape(devices, capacity, 2)
    code_rows = jnp.swapaxes(code_rows, 1, 2).astype(jnp.bfloat16)
    code_rows = jnp.pad(code_rows, ((0, 0), (0, EXTRA - 2), (0, width - capacity)))
    message = jnp.concatenate([send_rows, code_rows], axis=1)
    got = lax.all_to_all(message, ("cell", "own"), split_axis=0, concat_axis=0, tiled=True)
    lanes = capacity + EXTRA
    recv_rows = got.reshape(devices * lanes, width)
    high = got[:, capacity, :capacity].astype(jnp.int32)
    low = got[:, capacity + 1, :capacity].astype(jnp.int32)
    recv_cells = jnp.where(high > 0, (high - 1) * CODE + low, -1)
    recv_cells = jnp.pad(recv_cells, ((0, 0), (0, EXTRA)), constant_values=-1).reshape(devices * lanes)
    edges = jnp.concatenate(
        [jnp.arange(W, dtype=jnp.int32), jnp.arange(cells - W, cells, dtype=jnp.int32)]
    )
    edge_select = (recv_cells[:, None] == edges[None, :]).astype(jnp.bfloat16)
    edge_sum = lax.dot_general(
        recv_rows, edge_select, (((0,), (0,)), ((), ())), preferred_element_type=jnp.float32
    )
    edge_lev = smooth_levels(edge_sum.reshape(SPEC, width // SPEC, 2 * W))
    count = devices
    forward = [(i, i + 1) for i in range(count - 1)]
    backward = [(target, source) for source, target in forward]
    below = lax.ppermute(edge_lev[:, :, W:], ("cell", "own"), forward)
    above = lax.ppermute(edge_lev[:, :, :W], ("cell", "own"), backward)
    select = (recv_cells[:, None] == jnp.arange(cells, dtype=jnp.int32)[None, :]).astype(
        jnp.bfloat16
    )
    summed = lax.dot_general(
        recv_rows, select, (((0,), (0,)), ((), ())), preferred_element_type=jnp.float32
    )
    cellhist = summed.reshape(SPEC, width // SPEC, cells)
    weights = jnp.stack(
        [jnp.sum((offsets == shift).astype(jnp.float32), axis=0) for shift in range(-W, W + 1)]
    )
    rim = jnp.concatenate([below, above], axis=2)
    return fit_all(cellhist, rim, weights, MOM)


def solution(mesh):
    placed = (
        P(("cell", "own"), None, None),
        P(("cell", "own"), None),
        P(("cell", "own")),
        P(None, ("cell", "own")),
    )
    return jax.shard_map(
        body_inner,
        mesh=mesh,
        in_specs=placed,
        out_specs=(P(None, None, ("cell", "own")), P(None, ("cell", "own"))),
        check_vma=False,
    )
```

```python
import jax
import jax.numpy as jnp
import numpy as np
from jax import lax
from jax.experimental import pallas as pl
from jax.experimental.pallas import tpu as pltpu
from jax.sharding import PartitionSpec as P

SPEC = 2
MOM = 6
NEWTON = 8
W = 4
CODE = 32
EXTRA = 8
LOOP_PRECISION = lax.Precision.HIGH


def pair_list(count):
    return [(row, col) for row in range(count) for col in range(row + 1)]


def chol_solve(hess, rhs, count):
    lower = [[None] * count for _ in range(count)]
    for row in range(count):
        for col in range(row + 1):
            total = hess[row][col]
            for inner in range(col):
                total = total - lower[row][inner] * lower[col][inner]
            if row == col:
                lower[row][col] = jnp.sqrt(total)
            else:
                lower[row][col] = total / lower[col][col]
    forward = []
    for row in range(count):
        total = rhs[row]
        for inner in range(row):
            total = total - lower[row][inner] * forward[inner]
        forward.append(total / lower[row][row])
    backward = [None] * count
    for row in reversed(range(count)):
        total = forward[row]
        for inner in range(row + 1, count):
            total = total - lower[inner][row] * backward[inner]
        backward[row] = total / lower[row][row]
    return backward


def newton_step(got, moments, lam, count):
    pairs = pair_list(count)
    norm = got[count]
    first = [got[m] / norm for m in range(count)]
    hess = [[None] * count for _ in range(count)]
    for k, (row, col) in enumerate(pairs):
        second = got[count + 1 + k] / norm
        value = second - first[row] * first[col]
        if row == col:
            value = value + 0.01
        hess[row][col] = value
    rhs = [first[m] - moments[m] for m in range(count)]
    delta = chol_solve(hess, rhs, count)
    return [lam[m] - 0.5 * delta[m] for m in range(count)]


def fit_kernel(t_ref, phit_ref, psi_ref, lam_ref, fit_ref, lam_s, dense_ref):
    spec, levels, cells = t_ref.shape
    count = lam_ref.shape[0]
    used = count + 1 + len(pair_list(count))
    groups = 8 // spec
    part = cells // groups
    highest = lax.Precision.HIGHEST

    def contract(a, b, precision=highest):
        return jnp.dot(a, b, precision=precision, preferred_element_type=jnp.float32)

    def densify(gots):
        for s in range(spec):
            for j in range(groups):
                piece = gots[s][:, j * part : (j + 1) * part]
                row = s * groups + j
                for k in range(used):
                    dense_ref[k, row : row + 1, :] = piece[k : k + 1, :]
        return [dense_ref[k] for k in range(used)]

    def spread(values):
        for m in range(count):
            for s in range(spec):
                for j in range(groups):
                    row = s * groups + j
                    lam_s[s, m : m + 1, j * part : (j + 1) * part] = values[m][row : row + 1, :]

    got = densify([contract(psi_ref[...], t_ref[s]) for s in range(spec)])
    moments = [got[m] / got[count] for m in range(count)]
    lam_s[...] = jnp.zeros(lam_s.shape, jnp.float32)
    zero = jnp.zeros((8, part), jnp.float32)

    def step(_, lam):
        gots = []
        for s in range(spec):
            expo = jnp.exp(contract(phit_ref[...], lam_s[s], LOOP_PRECISION))
            gots.append(contract(psi_ref[...], expo, LOOP_PRECISION))
        new = newton_step(densify(gots), moments, list(lam), count)
        spread(new)
        return tuple(new)

    lax.fori_loop(0, NEWTON, step, tuple([zero] * count))
    for s in range(spec):
        target = t_ref[s]
        exponent = contract(phit_ref[...], lam_s[s])
        log_norm = jnp.log(jnp.sum(jnp.exp(exponent), axis=0, keepdims=True))
        whole = jnp.sum(target, axis=0, keepdims=True)
        ratio = jnp.log(target / whole) - (exponent - log_norm)
        fit_ref[s : s + 1, :] = 2.0 * jnp.sum(target * ratio, axis=0, keepdims=True) / levels
        for m in range(count):
            lam_ref[m, s : s + 1, :] = lam_s[s, m : m + 1, :]


def legendre_numpy(levels, count):
    xpos = (2.0 * np.arange(levels, dtype=np.float64) + 1.0) / levels - 1.0
    prev = np.ones_like(xpos)
    curr = xpos
    table = [curr]
    for order in range(1, count):
        nxt = ((2 * order + 1) * xpos * curr - order * prev) / (order + 1)
        prev, curr = (curr, nxt)
        table.append(curr)
    return np.stack(table, axis=0).astype(np.float32)


def fit_all(target, count):
    spec, levels, cells = target.shape
    phi = legendre_numpy(levels, count)
    pairs = pair_list(count)
    width = 8
    phit = np.zeros((levels, width), np.float32)
    phit[:, :count] = phi.T
    rows = [phi[m] for m in range(count)] + [np.ones((levels,), np.float32)]
    rows += [phi[r] * phi[c] for r, c in pairs]
    height = -(-len(rows) // 8) * 8
    rows += [np.zeros((levels,), np.float32)] * (height - len(rows))
    psi = np.stack(rows, axis=0)
    lam, fit = pl.pallas_call(
        fit_kernel,
        out_shape=(
            jax.ShapeDtypeStruct((count, spec, cells), jnp.float32),
            jax.ShapeDtypeStruct((spec, cells), jnp.float32),
        ),
        scratch_shapes=[
            pltpu.VMEM((spec, width, cells), jnp.float32),
            pltpu.VMEM((height, 8, cells * spec // 8), jnp.float32),
        ],
    )(target, jnp.asarray(phit), jnp.asarray(psi))
    return jnp.transpose(lam, (1, 0, 2)), fit


def smooth_levels(field):
    padded = jnp.pad(field, ((0, 0), (1, 1), (0, 0)))
    return 0.5 * field + 0.25 * (padded[:, :-2, :] + padded[:, 2:, :])


def body_inner(hist, dest, cell_in, offsets):
    rows = hist.shape[0]
    width = hist.shape[2]
    cells = offsets.shape[1]
    devices = lax.axis_size(("cell", "own"))
    capacity = 2 * rows // devices
    slots = devices * capacity
    packed = jnp.sum(hist, axis=1, dtype=jnp.float32).astype(jnp.bfloat16)
    target_block = dest[:, 0]
    member = (target_block[:, None] == jnp.arange(devices, dtype=jnp.int32)[None, :]).astype(
        jnp.int32
    )
    ranks = jnp.sum((jnp.cumsum(member, axis=0) - 1) * member, axis=1)
    position = target_block * capacity + ranks
    column = jnp.arange(128, dtype=jnp.int32)[None, :]
    codes = jnp.where(
        column == 0, cell_in[:, None] // CODE + 1, jnp.where(column == 1, cell_in[:, None] % CODE, 0)
    ).astype(jnp.bfloat16)
    payload = jnp.concatenate([packed, codes], axis=1)
    place = (jnp.arange(slots, dtype=jnp.int32)[:, None] == position[None, :]).astype(jnp.bfloat16)
    sent = jnp.dot(place, payload, preferred_element_type=jnp.float32)
    send_rows = sent[:, :width].astype(jnp.bfloat16).reshape(devices, capacity, width)
    code_rows = sent[:, width : width + 2].reshape(devices, capacity, 2)
    code_rows = jnp.swapaxes(code_rows, 1, 2).astype(jnp.bfloat16)
    code_rows = jnp.pad(code_rows, ((0, 0), (0, EXTRA - 2), (0, width - capacity)))
    message = jnp.concatenate([send_rows, code_rows], axis=1)
    got = lax.all_to_all(message, ("cell", "own"), split_axis=0, concat_axis=0, tiled=True)
    lanes = capacity + EXTRA
    recv_rows = got.reshape(devices * lanes, width)
    high = got[:, capacity, :capacity].astype(jnp.int32)
    low = got[:, capacity + 1, :capacity].astype(jnp.int32)
    recv_cells = jnp.where(high > 0, (high - 1) * CODE + low, -1)
    recv_cells = jnp.pad(recv_cells, ((0, 0), (0, EXTRA)), constant_values=-1).reshape(devices * lanes)
    edges = jnp.concatenate(
        [jnp.arange(W, dtype=jnp.int32), jnp.arange(cells - W, cells, dtype=jnp.int32)]
    )
    edge_select = (recv_cells[:, None] == edges[None, :]).astype(jnp.bfloat16)
    edge_sum = lax.dot_general(
        recv_rows, edge_select, (((0,), (0,)), ((), ())), preferred_element_type=jnp.float32
    )
    edge_lev = smooth_levels(edge_sum.reshape(SPEC, width // SPEC, 2 * W))
    count = devices
    forward = [(i, i + 1) for i in range(count - 1)]
    backward = [(target, source) for source, target in forward]
    below = lax.ppermute(edge_lev[:, :, W:], ("cell", "own"), forward)
    above = lax.ppermute(edge_lev[:, :, :W], ("cell", "own"), backward)
    select = (recv_cells[:, None] == jnp.arange(cells, dtype=jnp.int32)[None, :]).astype(
        jnp.bfloat16
    )
    summed = lax.dot_general(
        recv_rows, select, (((0,), (0,)), ((), ())), preferred_element_type=jnp.float32
    )
    cellhist = summed.reshape(SPEC, width // SPEC, cells)
    levelled = smooth_levels(cellhist)
    rimmed = jnp.concatenate([below, levelled, above], axis=2)
    target = 1.0 + levelled
    for shift in range(-W, W + 1):
        weight = jnp.sum((offsets == shift).astype(jnp.float32), axis=0)
        target = target + weight[None, None, :] * lax.slice_in_dim(
            rimmed, W + shift, W + shift + cells, axis=2
        )
    return fit_all(target, MOM)


def solution(mesh):
    placed = (
        P(("cell", "own"), None, None),
        P(("cell", "own"), None),
        P(("cell", "own")),
        P(None, ("cell", "own")),
    )
    return jax.shard_map(
        body_inner,
        mesh=mesh,
        in_specs=placed,
        out_specs=(P(None, None, ("cell", "own")), P(None, ("cell", "own"))),
        check_vma=False,
    )
```

```python
import jax
import jax.numpy as jnp
import numpy as np
from jax import lax
from jax.experimental import pallas as pl
from jax.experimental.pallas import tpu as pltpu
from jax.sharding import PartitionSpec as P

SPEC = 2
MOM = 6
NEWTON = 8
W = 4
CODE = 32
EXTRA = 8
LOOP_PRECISION = lax.Precision.HIGH


def pair_list(count):
    return [(row, col) for row in range(count) for col in range(row + 1)]


def chol_solve(hess, rhs, count):
    lower = [[None] * count for _ in range(count)]
    for row in range(count):
        for col in range(row + 1):
            total = hess[row][col]
            for inner in range(col):
                total = total - lower[row][inner] * lower[col][inner]
            if row == col:
                lower[row][col] = jnp.sqrt(total)
            else:
                lower[row][col] = total / lower[col][col]
    forward = []
    for row in range(count):
        total = rhs[row]
        for inner in range(row):
            total = total - lower[row][inner] * forward[inner]
        forward.append(total / lower[row][row])
    backward = [None] * count
    for row in reversed(range(count)):
        total = forward[row]
        for inner in range(row + 1, count):
            total = total - lower[inner][row] * backward[inner]
        backward[row] = total / lower[row][row]
    return backward


def newton_step(got, moments, lam, count):
    pairs = pair_list(count)
    norm = got[count]
    first = [got[m] / norm for m in range(count)]
    hess = [[None] * count for _ in range(count)]
    for k, (row, col) in enumerate(pairs):
        second = got[count + 1 + k] / norm
        value = second - first[row] * first[col]
        if row == col:
            value = value + 0.01
        hess[row][col] = value
    rhs = [first[m] - moments[m] for m in range(count)]
    delta = chol_solve(hess, rhs, count)
    return [lam[m] - 0.5 * delta[m] for m in range(count)]


def fit_kernel(t_ref, phit_ref, psi_ref, lam_ref, fit_ref, lam_s, dense_ref):
    spec, levels, cells = t_ref.shape
    count = lam_ref.shape[0]
    used = count + 1 + len(pair_list(count))
    groups = 8 // spec
    part = cells // groups
    highest = lax.Precision.HIGHEST

    def contract(a, b, precision=highest):
        return jnp.dot(a, b, precision=precision, preferred_element_type=jnp.float32)

    def densify(gots):
        for s in range(spec):
            for j in range(groups):
                piece = gots[s][:, j * part : (j + 1) * part]
                row = s * groups + j
                for k in range(used):
                    dense_ref[k, row : row + 1, :] = piece[k : k + 1, :]
        return [dense_ref[k] for k in range(used)]

    def spread(values):
        for m in range(count):
            for s in range(spec):
                for j in range(groups):
                    row = s * groups + j
                    lam_s[s, m : m + 1, j * part : (j + 1) * part] = values[m][row : row + 1, :]

    got = densify([contract(psi_ref[...], t_ref[s]) for s in range(spec)])
    moments = [got[m] / got[count] for m in range(count)]
    lam_s[...] = jnp.zeros(lam_s.shape, jnp.float32)
    zero = jnp.zeros((8, part), jnp.float32)

    def step(_, lam):
        gots = []
        for s in range(spec):
            expo = jnp.exp(contract(phit_ref[...], lam_s[s], LOOP_PRECISION))
            gots.append(contract(psi_ref[...], expo, LOOP_PRECISION))
        new = newton_step(densify(gots), moments, list(lam), count)
        spread(new)
        return tuple(new)

    lax.fori_loop(0, NEWTON, step, tuple([zero] * count))
    for s in range(spec):
        target = t_ref[s]
        exponent = contract(phit_ref[...], lam_s[s])
        log_norm = jnp.log(jnp.sum(jnp.exp(exponent), axis=0, keepdims=True))
        whole = jnp.sum(target, axis=0, keepdims=True)
        ratio = jnp.log(target / whole) - (exponent - log_norm)
        fit_ref[s : s + 1, :] = 2.0 * jnp.sum(target * ratio, axis=0, keepdims=True) / levels
        for m in range(count):
            lam_ref[m, s : s + 1, :] = lam_s[s, m : m + 1, :]


def legendre_numpy(levels, count):
    xpos = (2.0 * np.arange(levels, dtype=np.float64) + 1.0) / levels - 1.0
    prev = np.ones_like(xpos)
    curr = xpos
    table = [curr]
    for order in range(1, count):
        nxt = ((2 * order + 1) * xpos * curr - order * prev) / (order + 1)
        prev, curr = (curr, nxt)
        table.append(curr)
    return np.stack(table, axis=0).astype(np.float32)


def fit_all(target, count):
    spec, levels, cells = target.shape
    phi = legendre_numpy(levels, count)
    pairs = pair_list(count)
    width = 8
    phit = np.zeros((levels, width), np.float32)
    phit[:, :count] = phi.T
    rows = [phi[m] for m in range(count)] + [np.ones((levels,), np.float32)]
    rows += [phi[r] * phi[c] for r, c in pairs]
    height = -(-len(rows) // 8) * 8
    rows += [np.zeros((levels,), np.float32)] * (height - len(rows))
    psi = np.stack(rows, axis=0)
    lam, fit = pl.pallas_call(
        fit_kernel,
        out_shape=(
            jax.ShapeDtypeStruct((count, spec, cells), jnp.float32),
            jax.ShapeDtypeStruct((spec, cells), jnp.float32),
        ),
        scratch_shapes=[
            pltpu.VMEM((spec, width, cells), jnp.float32),
            pltpu.VMEM((height, 8, cells * spec // 8), jnp.float32),
        ],
    )(target, jnp.asarray(phit), jnp.asarray(psi))
    return jnp.transpose(lam, (1, 0, 2)), fit


def smooth_levels(field):
    padded = jnp.pad(field, ((0, 0), (1, 1), (0, 0)))
    return 0.5 * field + 0.25 * (padded[:, :-2, :] + padded[:, 2:, :])


def body_inner(hist, dest, cell_in, offsets):
    rows = hist.shape[0]
    width = hist.shape[2]
    cells = offsets.shape[1]
    devices = lax.axis_size(("cell", "own"))
    capacity = 2 * rows // devices
    slots = devices * capacity
    packed = jnp.sum(hist, axis=1, dtype=jnp.float32).astype(jnp.bfloat16)
    target_block = dest[:, 0]
    member = (target_block[:, None] == jnp.arange(devices, dtype=jnp.int32)[None, :]).astype(
        jnp.int32
    )
    ranks = jnp.sum((jnp.cumsum(member, axis=0) - 1) * member, axis=1)
    position = target_block * capacity + ranks
    codes = jnp.stack([cell_in // CODE + 1, cell_in % CODE], axis=1).astype(jnp.bfloat16)
    codes = jnp.pad(codes, ((0, 0), (0, 128 - 2)))
    payload = jnp.concatenate([packed, codes], axis=1)
    place = (jnp.arange(slots, dtype=jnp.int32)[:, None] == position[None, :]).astype(jnp.bfloat16)
    sent = jnp.dot(place, payload, preferred_element_type=jnp.float32)
    send_rows = sent[:, :width].astype(jnp.bfloat16).reshape(devices, capacity, width)
    code_rows = sent[:, width : width + 2].reshape(devices, capacity, 2)
    code_rows = jnp.swapaxes(code_rows, 1, 2).astype(jnp.bfloat16)
    narrow = 128
    split = width // narrow
    code_rows = jnp.pad(code_rows, ((0, 0), (0, EXTRA - 2), (0, narrow - capacity)))
    message = jnp.concatenate(
        [send_rows.reshape(devices, capacity * split, narrow), code_rows], axis=1
    )
    got = lax.all_to_all(message, ("cell", "own"), split_axis=0, concat_axis=0, tiled=True)
    lanes = capacity + EXTRA // split
    recv_rows = got.reshape(devices * lanes, width)
    high = got[:, capacity * split, :capacity].astype(jnp.int32)
    low = got[:, capacity * split + 1, :capacity].astype(jnp.int32)
    recv_cells = jnp.where(high > 0, (high - 1) * CODE + low, -1)
    recv_cells = jnp.pad(recv_cells, ((0, 0), (0, lanes - capacity)), constant_values=-1)
    recv_cells = recv_cells.reshape(devices * lanes)
    edges = jnp.concatenate(
        [jnp.arange(W, dtype=jnp.int32), jnp.arange(cells - W, cells, dtype=jnp.int32)]
    )
    edge_select = (recv_cells[:, None] == edges[None, :]).astype(jnp.bfloat16)
    edge_sum = lax.dot_general(
        recv_rows, edge_select, (((0,), (0,)), ((), ())), preferred_element_type=jnp.float32
    )
    edge_lev = smooth_levels(edge_sum.reshape(SPEC, width // SPEC, 2 * W))
    count = devices
    forward = [(i, i + 1) for i in range(count - 1)]
    backward = [(target, source) for source, target in forward]
    below = lax.ppermute(edge_lev[:, :, W:], ("cell", "own"), forward)
    above = lax.ppermute(edge_lev[:, :, :W], ("cell", "own"), backward)
    select = (recv_cells[:, None] == jnp.arange(cells, dtype=jnp.int32)[None, :]).astype(
        jnp.bfloat16
    )
    summed = lax.dot_general(
        recv_rows, select, (((0,), (0,)), ((), ())), preferred_element_type=jnp.float32
    )
    cellhist = summed.reshape(SPEC, width // SPEC, cells)
    levelled = smooth_levels(cellhist)
    rimmed = jnp.concatenate([below, levelled, above], axis=2)
    target = 1.0 + levelled
    for shift in range(-W, W + 1):
        weight = jnp.sum((offsets == shift).astype(jnp.float32), axis=0)
        target = target + weight[None, None, :] * lax.slice_in_dim(
            rimmed, W + shift, W + shift + cells, axis=2
        )
    return fit_all(target, MOM)


def solution(mesh):
    placed = (
        P(("cell", "own"), None, None),
        P(("cell", "own"), None),
        P(("cell", "own")),
        P(None, ("cell", "own")),
    )
    return jax.shard_map(
        body_inner,
        mesh=mesh,
        in_specs=placed,
        out_specs=(P(None, None, ("cell", "own")), P(None, ("cell", "own"))),
        check_vma=False,
    )
```

```python
import jax
import jax.numpy as jnp
import numpy as np
from jax import lax
from jax.experimental import pallas as pl
from jax.experimental.pallas import tpu as pltpu
from jax.sharding import PartitionSpec as P

SPEC = 2
MOM = 6
NEWTON = 8
W = 4
CODE = 32
EXTRA = 8
LOOP_PRECISION = lax.Precision.HIGH


def pair_list(count):
    return [(row, col) for row in range(count) for col in range(row + 1)]


def chol_solve(hess, rhs, count):
    lower = [[None] * count for _ in range(count)]
    for row in range(count):
        for col in range(row + 1):
            total = hess[row][col]
            for inner in range(col):
                total = total - lower[row][inner] * lower[col][inner]
            if row == col:
                lower[row][col] = jnp.sqrt(total)
            else:
                lower[row][col] = total / lower[col][col]
    forward = []
    for row in range(count):
        total = rhs[row]
        for inner in range(row):
            total = total - lower[row][inner] * forward[inner]
        forward.append(total / lower[row][row])
    backward = [None] * count
    for row in reversed(range(count)):
        total = forward[row]
        for inner in range(row + 1, count):
            total = total - lower[inner][row] * backward[inner]
        backward[row] = total / lower[row][row]
    return backward


def newton_step(got, moments, lam, count):
    pairs = pair_list(count)
    norm = got[count]
    first = [got[m] / norm for m in range(count)]
    hess = [[None] * count for _ in range(count)]
    for k, (row, col) in enumerate(pairs):
        second = got[count + 1 + k] / norm
        value = second - first[row] * first[col]
        if row == col:
            value = value + 0.01
        hess[row][col] = value
    rhs = [first[m] - moments[m] for m in range(count)]
    delta = chol_solve(hess, rhs, count)
    return [lam[m] - 0.5 * delta[m] for m in range(count)]


def fit_kernel(t_ref, phit_ref, psi_ref, lam_ref, fit_ref, lam_s, dense_ref):
    spec, levels, cells = t_ref.shape
    count = lam_ref.shape[0]
    used = count + 1 + len(pair_list(count))
    groups = 8 // spec
    part = cells // groups
    highest = lax.Precision.HIGHEST

    def contract(a, b, precision=highest):
        return jnp.dot(a, b, precision=precision, preferred_element_type=jnp.float32)

    def densify(gots):
        for s in range(spec):
            for j in range(groups):
                piece = gots[s][:, j * part : (j + 1) * part]
                row = s * groups + j
                for k in range(used):
                    dense_ref[k, row : row + 1, :] = piece[k : k + 1, :]
        return [dense_ref[k] for k in range(used)]

    def spread(values):
        for m in range(count):
            for s in range(spec):
                for j in range(groups):
                    row = s * groups + j
                    lam_s[s, m : m + 1, j * part : (j + 1) * part] = values[m][row : row + 1, :]

    got = densify([contract(psi_ref[...], t_ref[s]) for s in range(spec)])
    moments = [got[m] / got[count] for m in range(count)]
    lam_s[...] = jnp.zeros(lam_s.shape, jnp.float32)
    zero = jnp.zeros((8, part), jnp.float32)

    def step(_, lam):
        gots = []
        for s in range(spec):
            expo = jnp.exp(contract(phit_ref[...], lam_s[s], LOOP_PRECISION))
            gots.append(contract(psi_ref[...], expo, LOOP_PRECISION))
        new = newton_step(densify(gots), moments, list(lam), count)
        spread(new)
        return tuple(new)

    lax.fori_loop(0, NEWTON, step, tuple([zero] * count))
    for s in range(spec):
        target = t_ref[s]
        exponent = contract(phit_ref[...], lam_s[s])
        log_norm = jnp.log(jnp.sum(jnp.exp(exponent), axis=0, keepdims=True))
        whole = jnp.sum(target, axis=0, keepdims=True)
        ratio = jnp.log(target / whole) - (exponent - log_norm)
        fit_ref[s : s + 1, :] = 2.0 * jnp.sum(target * ratio, axis=0, keepdims=True) / levels
        for m in range(count):
            lam_ref[m, s : s + 1, :] = lam_s[s, m : m + 1, :]


def legendre_numpy(levels, count):
    xpos = (2.0 * np.arange(levels, dtype=np.float64) + 1.0) / levels - 1.0
    prev = np.ones_like(xpos)
    curr = xpos
    table = [curr]
    for order in range(1, count):
        nxt = ((2 * order + 1) * xpos * curr - order * prev) / (order + 1)
        prev, curr = (curr, nxt)
        table.append(curr)
    return np.stack(table, axis=0).astype(np.float32)


def fit_all(target, count):
    spec, levels, cells = target.shape
    phi = legendre_numpy(levels, count)
    pairs = pair_list(count)
    width = 8
    phit = np.zeros((levels, width), np.float32)
    phit[:, :count] = phi.T
    rows = [phi[m] for m in range(count)] + [np.ones((levels,), np.float32)]
    rows += [phi[r] * phi[c] for r, c in pairs]
    height = -(-len(rows) // 8) * 8
    rows += [np.zeros((levels,), np.float32)] * (height - len(rows))
    psi = np.stack(rows, axis=0)
    lam, fit = pl.pallas_call(
        fit_kernel,
        out_shape=(
            jax.ShapeDtypeStruct((count, spec, cells), jnp.float32),
            jax.ShapeDtypeStruct((spec, cells), jnp.float32),
        ),
        scratch_shapes=[
            pltpu.VMEM((spec, width, cells), jnp.float32),
            pltpu.VMEM((height, 8, cells * spec // 8), jnp.float32),
        ],
    )(target, jnp.asarray(phit), jnp.asarray(psi))
    return jnp.transpose(lam, (1, 0, 2)), fit


def smooth_levels(field):
    padded = jnp.pad(field, ((0, 0), (1, 1), (0, 0)))
    return 0.5 * field + 0.25 * (padded[:, :-2, :] + padded[:, 2:, :])


def body_inner(hist, dest, cell_in, offsets):
    rows = hist.shape[0]
    width = hist.shape[2]
    cells = offsets.shape[1]
    devices = lax.axis_size(("cell", "own"))
    capacity = 2 * rows // devices
    slots = devices * capacity
    packed = jnp.sum(hist, axis=1, dtype=jnp.float32).astype(jnp.bfloat16)
    target_block = dest[:, 0]
    member = (target_block[:, None] == jnp.arange(devices, dtype=jnp.int32)[None, :]).astype(
        jnp.int32
    )
    ranks = jnp.sum((jnp.cumsum(member, axis=0) - 1) * member, axis=1)
    position = target_block * capacity + ranks
    codes = jnp.stack([cell_in // CODE + 1, cell_in % CODE], axis=1).astype(jnp.bfloat16)
    codes = jnp.pad(codes, ((0, 0), (0, 128 - 2)))
    payload = jnp.concatenate([packed, codes], axis=1)
    place = (jnp.arange(slots, dtype=jnp.int32)[:, None] == position[None, :]).astype(jnp.bfloat16)
    sent = jnp.dot(place, payload, preferred_element_type=jnp.float32)
    narrow = width // SPEC
    halves = [
        sent[:, h * narrow : (h + 1) * narrow].astype(jnp.bfloat16).reshape(devices, capacity, narrow)
        for h in range(SPEC)
    ]
    code_rows = sent[:, width : width + 2].reshape(devices, capacity, 2)
    code_rows = jnp.swapaxes(code_rows, 1, 2).astype(jnp.bfloat16)
    code_rows = jnp.pad(code_rows, ((0, 0), (0, EXTRA - 2), (0, narrow - capacity)))
    message = jnp.concatenate(halves + [code_rows], axis=1)
    got = lax.all_to_all(message, ("cell", "own"), split_axis=0, concat_axis=0, tiled=True)
    recv_halves = [
        got[:, h * capacity : (h + 1) * capacity, :].reshape(slots, narrow) for h in range(SPEC)
    ]
    high = got[:, SPEC * capacity, :capacity].astype(jnp.int32).reshape(slots)
    low = got[:, SPEC * capacity + 1, :capacity].astype(jnp.int32).reshape(slots)
    recv_cells = jnp.where(high > 0, (high - 1) * CODE + low, -1)

    def cell_sums(picked):
        return jnp.stack(
            [
                lax.dot_general(
                    part, picked, (((0,), (0,)), ((), ())), preferred_element_type=jnp.float32
                )
                for part in recv_halves
            ]
        )

    edges = jnp.concatenate(
        [jnp.arange(W, dtype=jnp.int32), jnp.arange(cells - W, cells, dtype=jnp.int32)]
    )
    edge_lev = smooth_levels(cell_sums((recv_cells[:, None] == edges[None, :]).astype(jnp.bfloat16)))
    forward = [(i, i + 1) for i in range(devices - 1)]
    backward = [(target, source) for source, target in forward]
    below = lax.ppermute(edge_lev[:, :, W:], ("cell", "own"), forward)
    above = lax.ppermute(edge_lev[:, :, :W], ("cell", "own"), backward)
    select = (recv_cells[:, None] == jnp.arange(cells, dtype=jnp.int32)[None, :]).astype(
        jnp.bfloat16
    )
    cellhist = cell_sums(select)
    levelled = smooth_levels(cellhist)
    rimmed = jnp.concatenate([below, levelled, above], axis=2)
    target = 1.0 + levelled
    for shift in range(-W, W + 1):
        weight = jnp.sum((offsets == shift).astype(jnp.float32), axis=0)
        target = target + weight[None, None, :] * lax.slice_in_dim(
            rimmed, W + shift, W + shift + cells, axis=2
        )
    return fit_all(target, MOM)


def solution(mesh):
    placed = (
        P(("cell", "own"), None, None),
        P(("cell", "own"), None),
        P(("cell", "own")),
        P(None, ("cell", "own")),
    )
    return jax.shard_map(
        body_inner,
        mesh=mesh,
        in_specs=placed,
        out_specs=(P(None, None, ("cell", "own")), P(None, ("cell", "own"))),
        check_vma=False,
    )
```

```python
import jax
import jax.numpy as jnp
import numpy as np
from jax import lax
from jax.experimental import pallas as pl
from jax.experimental.pallas import tpu as pltpu
from jax.sharding import PartitionSpec as P

SPEC = 2
MOM = 6
NEWTON = 8
W = 4
CODE = 32
EXTRA = 8
LOOP_PRECISION = lax.Precision.HIGH


def pair_list(count):
    return [(row, col) for row in range(count) for col in range(row + 1)]


def chol_solve(hess, rhs, count):
    lower = [[None] * count for _ in range(count)]
    for row in range(count):
        for col in range(row + 1):
            total = hess[row][col]
            for inner in range(col):
                total = total - lower[row][inner] * lower[col][inner]
            if row == col:
                lower[row][col] = jnp.sqrt(total)
            else:
                lower[row][col] = total / lower[col][col]
    forward = []
    for row in range(count):
        total = rhs[row]
        for inner in range(row):
            total = total - lower[row][inner] * forward[inner]
        forward.append(total / lower[row][row])
    backward = [None] * count
    for row in reversed(range(count)):
        total = forward[row]
        for inner in range(row + 1, count):
            total = total - lower[inner][row] * backward[inner]
        backward[row] = total / lower[row][row]
    return backward


def newton_step(got, moments, lam, count):
    pairs = pair_list(count)
    norm = got[count]
    first = [got[m] / norm for m in range(count)]
    hess = [[None] * count for _ in range(count)]
    for k, (row, col) in enumerate(pairs):
        second = got[count + 1 + k] / norm
        value = second - first[row] * first[col]
        if row == col:
            value = value + 0.01
        hess[row][col] = value
    rhs = [first[m] - moments[m] for m in range(count)]
    delta = chol_solve(hess, rhs, count)
    return [lam[m] - 0.5 * delta[m] for m in range(count)]


def fit_kernel(
    h0_ref, h1_ref, below_ref, above_ref, w_ref, phit_ref, psi_ref, lam_ref, fit_ref, lam_s,
    dense_ref, t_ref, ext_ref,
):
    spec, levels, cells = t_ref.shape
    h_refs = (h0_ref, h1_ref)
    pad = (ext_ref.shape[2] - cells) // 2
    rim = below_ref.shape[2]
    ext_ref[...] = jnp.zeros(ext_ref.shape, jnp.float32)
    for s in range(spec):
        field = h_refs[s][...]
        t_ref[s] = field
        lower = jnp.concatenate([jnp.zeros((1, cells), jnp.float32), t_ref[s, : levels - 1, :]], axis=0)
        upper = jnp.concatenate([t_ref[s, 1:, :], jnp.zeros((1, cells), jnp.float32)], axis=0)
        levelled = 0.5 * field + 0.25 * (lower + upper)
        ext_ref[s, :, pad : pad + cells] = levelled
        ext_ref[s, :, pad - rim : pad] = below_ref[s]
        ext_ref[s, :, pad + cells : pad + cells + rim] = above_ref[s]
        target = 1.0 + levelled
        for k in range(w_ref.shape[0]):
            shift = k - w_ref.shape[0] // 2
            target = target + w_ref[k : k + 1, :] * ext_ref[s, :, pad + shift : pad + shift + cells]
        t_ref[s] = target
    count = lam_ref.shape[0]
    used = count + 1 + len(pair_list(count))
    groups = 8 // spec
    part = cells // groups
    highest = lax.Precision.HIGHEST

    def contract(a, b, precision=highest):
        return jnp.dot(a, b, precision=precision, preferred_element_type=jnp.float32)

    def densify(gots):
        for s in range(spec):
            for j in range(groups):
                piece = gots[s][:, j * part : (j + 1) * part]
                row = s * groups + j
                for k in range(used):
                    dense_ref[k, row : row + 1, :] = piece[k : k + 1, :]
        return [dense_ref[k] for k in range(used)]

    def spread(values):
        for m in range(count):
            for s in range(spec):
                for j in range(groups):
                    row = s * groups + j
                    lam_s[s, m : m + 1, j * part : (j + 1) * part] = values[m][row : row + 1, :]

    got = densify([contract(psi_ref[...], t_ref[s]) for s in range(spec)])
    moments = [got[m] / got[count] for m in range(count)]
    lam_s[...] = jnp.zeros(lam_s.shape, jnp.float32)
    zero = jnp.zeros((8, part), jnp.float32)

    def step(_, lam):
        gots = []
        for s in range(spec):
            expo = jnp.exp(contract(phit_ref[...], lam_s[s], LOOP_PRECISION))
            gots.append(contract(psi_ref[...], expo, LOOP_PRECISION))
        new = newton_step(densify(gots), moments, list(lam), count)
        spread(new)
        return tuple(new)

    lax.fori_loop(0, NEWTON, step, tuple([zero] * count))
    for s in range(spec):
        target = t_ref[s]
        exponent = contract(phit_ref[...], lam_s[s])
        log_norm = jnp.log(jnp.sum(jnp.exp(exponent), axis=0, keepdims=True))
        whole = jnp.sum(target, axis=0, keepdims=True)
        ratio = jnp.log(target / whole) - (exponent - log_norm)
        fit_ref[s : s + 1, :] = 2.0 * jnp.sum(target * ratio, axis=0, keepdims=True) / levels
        for m in range(count):
            lam_ref[m, s : s + 1, :] = lam_s[s, m : m + 1, :]


def legendre_numpy(levels, count):
    xpos = (2.0 * np.arange(levels, dtype=np.float64) + 1.0) / levels - 1.0
    prev = np.ones_like(xpos)
    curr = xpos
    table = [curr]
    for order in range(1, count):
        nxt = ((2 * order + 1) * xpos * curr - order * prev) / (order + 1)
        prev, curr = (curr, nxt)
        table.append(curr)
    return np.stack(table, axis=0).astype(np.float32)


def fit_all(hists, below, above, weights, count):
    spec = len(hists)
    levels, cells = hists[0].shape
    phi = legendre_numpy(levels, count)
    pairs = pair_list(count)
    width = 8
    phit = np.zeros((levels, width), np.float32)
    phit[:, :count] = phi.T
    rows = [phi[m] for m in range(count)] + [np.ones((levels,), np.float32)]
    rows += [phi[r] * phi[c] for r, c in pairs]
    height = -(-len(rows) // 8) * 8
    rows += [np.zeros((levels,), np.float32)] * (height - len(rows))
    psi = np.stack(rows, axis=0)
    lam, fit = pl.pallas_call(
        fit_kernel,
        out_shape=(
            jax.ShapeDtypeStruct((count, spec, cells), jnp.float32),
            jax.ShapeDtypeStruct((spec, cells), jnp.float32),
        ),
        scratch_shapes=[
            pltpu.VMEM((spec, width, cells), jnp.float32),
            pltpu.VMEM((height, 8, cells * spec // 8), jnp.float32),
            pltpu.VMEM((spec, levels, cells), jnp.float32),
            pltpu.VMEM((spec, levels, cells + 256), jnp.float32),
        ],
    )(*hists, below, above, weights, jnp.asarray(phit), jnp.asarray(psi))
    return jnp.transpose(lam, (1, 0, 2)), fit


def smooth_levels(field):
    padded = jnp.pad(field, ((0, 0), (1, 1), (0, 0)))
    return 0.5 * field + 0.25 * (padded[:, :-2, :] + padded[:, 2:, :])


def body_inner(hist, dest, cell_in, offsets):
    rows = hist.shape[0]
    width = hist.shape[2]
    cells = offsets.shape[1]
    devices = lax.axis_size(("cell", "own"))
    capacity = 2 * rows // devices
    slots = devices * capacity
    packed = jnp.sum(hist, axis=1, dtype=jnp.float32).astype(jnp.bfloat16)
    target_block = dest[:, 0]
    member = (target_block[:, None] == jnp.arange(devices, dtype=jnp.int32)[None, :]).astype(
        jnp.int32
    )
    ranks = jnp.sum((jnp.cumsum(member, axis=0) - 1) * member, axis=1)
    position = target_block * capacity + ranks
    codes = jnp.stack([cell_in // CODE + 1, cell_in % CODE], axis=1).astype(jnp.bfloat16)
    codes = jnp.pad(codes, ((0, 0), (0, 128 - 2)))
    payload = jnp.concatenate([packed, codes], axis=1)
    place = (jnp.arange(slots, dtype=jnp.int32)[:, None] == position[None, :]).astype(jnp.bfloat16)
    sent = jnp.dot(place, payload, preferred_element_type=jnp.float32)
    narrow = width // SPEC
    halves = [
        sent[:, h * narrow : (h + 1) * narrow].astype(jnp.bfloat16).reshape(devices, capacity, narrow)
        for h in range(SPEC)
    ]
    code_rows = sent[:, width : width + 2].reshape(devices, capacity, 2)
    code_rows = jnp.swapaxes(code_rows, 1, 2).astype(jnp.bfloat16)
    code_rows = jnp.pad(code_rows, ((0, 0), (0, EXTRA - 2), (0, narrow - capacity)))
    message = jnp.concatenate(halves + [code_rows], axis=1)
    got = lax.all_to_all(message, ("cell", "own"), split_axis=0, concat_axis=0, tiled=True)
    recv_halves = [
        got[:, h * capacity : (h + 1) * capacity, :].reshape(slots, narrow) for h in range(SPEC)
    ]
    high = got[:, SPEC * capacity, :capacity].astype(jnp.int32).reshape(slots)
    low = got[:, SPEC * capacity + 1, :capacity].astype(jnp.int32).reshape(slots)
    recv_cells = jnp.where(high > 0, (high - 1) * CODE + low, -1)

    def cell_sums(picked):
        return [
            lax.dot_general(
                part, picked, (((0,), (0,)), ((), ())), preferred_element_type=jnp.float32
            )
            for part in recv_halves
        ]

    edges = jnp.concatenate(
        [jnp.arange(W, dtype=jnp.int32), jnp.arange(cells - W, cells, dtype=jnp.int32)]
    )
    edge_lev = smooth_levels(
        jnp.stack(cell_sums((recv_cells[:, None] == edges[None, :]).astype(jnp.bfloat16)))
    )
    forward = [(i, i + 1) for i in range(devices - 1)]
    backward = [(target, source) for source, target in forward]
    below = lax.ppermute(edge_lev[:, :, W:], ("cell", "own"), forward)
    above = lax.ppermute(edge_lev[:, :, :W], ("cell", "own"), backward)
    select = (recv_cells[:, None] == jnp.arange(cells, dtype=jnp.int32)[None, :]).astype(
        jnp.bfloat16
    )
    cellhist = cell_sums(select)
    weights = jnp.stack(
        [jnp.sum((offsets == shift).astype(jnp.float32), axis=0) for shift in range(-W, W + 1)]
    )
    return fit_all(cellhist, below, above, weights, MOM)


def solution(mesh):
    placed = (
        P(("cell", "own"), None, None),
        P(("cell", "own"), None),
        P(("cell", "own")),
        P(None, ("cell", "own")),
    )
    return jax.shard_map(
        body_inner,
        mesh=mesh,
        in_specs=placed,
        out_specs=(P(None, None, ("cell", "own")), P(None, ("cell", "own"))),
        check_vma=False,
    )
```

```python
import jax
import jax.numpy as jnp
import numpy as np
from jax import lax
from jax.experimental import pallas as pl
from jax.experimental.pallas import tpu as pltpu
from jax.sharding import PartitionSpec as P

SPEC = 2
MOM = 6
NEWTON = 8
W = 4
CODE = 32
EXTRA = 8
LOOP_PRECISION = lax.Precision.HIGH


def pair_list(count):
    return [(row, col) for row in range(count) for col in range(row + 1)]


def chol_solve(hess, rhs, count):
    lower = [[None] * count for _ in range(count)]
    for row in range(count):
        for col in range(row + 1):
            total = hess[row][col]
            for inner in range(col):
                total = total - lower[row][inner] * lower[col][inner]
            if row == col:
                lower[row][col] = jnp.sqrt(total)
            else:
                lower[row][col] = total / lower[col][col]
    forward = []
    for row in range(count):
        total = rhs[row]
        for inner in range(row):
            total = total - lower[row][inner] * forward[inner]
        forward.append(total / lower[row][row])
    backward = [None] * count
    for row in reversed(range(count)):
        total = forward[row]
        for inner in range(row + 1, count):
            total = total - lower[inner][row] * backward[inner]
        backward[row] = total / lower[row][row]
    return backward


def newton_step(got, moments, lam, count):
    pairs = pair_list(count)
    norm = got[count]
    first = [got[m] / norm for m in range(count)]
    hess = [[None] * count for _ in range(count)]
    for k, (row, col) in enumerate(pairs):
        second = got[count + 1 + k] / norm
        value = second - first[row] * first[col]
        if row == col:
            value = value + 0.01
        hess[row][col] = value
    rhs = [first[m] - moments[m] for m in range(count)]
    delta = chol_solve(hess, rhs, count)
    return [lam[m] - 0.5 * delta[m] for m in range(count)]


def fit_kernel(
    h_ref, rim_ref, w_ref, phit_ref, psi_ref, lam_ref, fit_ref, lam_s, dense_ref, t_ref, ext_ref
):
    spec, levels, cells = h_ref.shape
    pad = (ext_ref.shape[2] - cells) // 2
    rim = rim_ref.shape[2] // 2
    ext_ref[...] = jnp.zeros(ext_ref.shape, jnp.float32)
    for s in range(spec):
        field = h_ref[s]
        t_ref[s] = field
        lower = jnp.concatenate([jnp.zeros((1, cells), jnp.float32), t_ref[s, : levels - 1, :]], axis=0)
        upper = jnp.concatenate([t_ref[s, 1:, :], jnp.zeros((1, cells), jnp.float32)], axis=0)
        levelled = 0.5 * field + 0.25 * (lower + upper)
        ext_ref[s, :, pad : pad + cells] = levelled
        ext_ref[s, :, pad - rim : pad] = rim_ref[s, :, :rim]
        ext_ref[s, :, pad + cells : pad + cells + rim] = rim_ref[s, :, rim:]
        target = 1.0 + levelled
        for k in range(w_ref.shape[0]):
            shift = k - w_ref.shape[0] // 2
            target = target + w_ref[k : k + 1, :] * ext_ref[s, :, pad + shift : pad + shift + cells]
        t_ref[s] = target
    count = lam_ref.shape[0]
    used = count + 1 + len(pair_list(count))
    groups = 8 // spec
    part = cells // groups
    highest = lax.Precision.HIGHEST

    def contract(a, b, precision=highest):
        return jnp.dot(a, b, precision=precision, preferred_element_type=jnp.float32)

    def densify(gots):
        for s in range(spec):
            for j in range(groups):
                piece = gots[s][:, j * part : (j + 1) * part]
                row = s * groups + j
                for k in range(used):
                    dense_ref[k, row : row + 1, :] = piece[k : k + 1, :]
        return [dense_ref[k] for k in range(used)]

    def spread(values):
        for m in range(count):
            for s in range(spec):
                for j in range(groups):
                    row = s * groups + j
                    lam_s[s, m : m + 1, j * part : (j + 1) * part] = values[m][row : row + 1, :]

    got = densify([contract(psi_ref[...], t_ref[s], LOOP_PRECISION) for s in range(spec)])
    moments = [got[m] / got[count] for m in range(count)]
    lam_s[...] = jnp.zeros(lam_s.shape, jnp.float32)
    zero = jnp.zeros((8, part), jnp.float32)

    def step(_, lam):
        gots = []
        for s in range(spec):
            expo = jnp.exp(contract(phit_ref[...], lam_s[s], LOOP_PRECISION))
            gots.append(contract(psi_ref[...], expo, LOOP_PRECISION))
        new = newton_step(densify(gots), moments, list(lam), count)
        spread(new)
        return tuple(new)

    lax.fori_loop(0, NEWTON, step, tuple([zero] * count))
    for s in range(spec):
        target = t_ref[s]
        exponent = contract(phit_ref[...], lam_s[s])
        log_norm = jnp.log(jnp.sum(jnp.exp(exponent), axis=0, keepdims=True))
        whole = jnp.sum(target, axis=0, keepdims=True)
        ratio = jnp.log(target / whole) - (exponent - log_norm)
        fit_ref[s : s + 1, :] = 2.0 * jnp.sum(target * ratio, axis=0, keepdims=True) / levels
        for m in range(count):
            lam_ref[m, s : s + 1, :] = lam_s[s, m : m + 1, :]


def legendre_numpy(levels, count):
    xpos = (2.0 * np.arange(levels, dtype=np.float64) + 1.0) / levels - 1.0
    prev = np.ones_like(xpos)
    curr = xpos
    table = [curr]
    for order in range(1, count):
        nxt = ((2 * order + 1) * xpos * curr - order * prev) / (order + 1)
        prev, curr = (curr, nxt)
        table.append(curr)
    return np.stack(table, axis=0).astype(np.float32)


def fit_all(cellhist, rim, weights, count):
    spec, levels, cells = cellhist.shape
    phi = legendre_numpy(levels, count)
    pairs = pair_list(count)
    width = 8
    phit = np.zeros((levels, width), np.float32)
    phit[:, :count] = phi.T
    rows = [phi[m] for m in range(count)] + [np.ones((levels,), np.float32)]
    rows += [phi[r] * phi[c] for r, c in pairs]
    height = -(-len(rows) // 8) * 8
    rows += [np.zeros((levels,), np.float32)] * (height - len(rows))
    psi = np.stack(rows, axis=0)
    lam, fit = pl.pallas_call(
        fit_kernel,
        out_shape=(
            jax.ShapeDtypeStruct((count, spec, cells), jnp.float32),
            jax.ShapeDtypeStruct((spec, cells), jnp.float32),
        ),
        scratch_shapes=[
            pltpu.VMEM((spec, width, cells), jnp.float32),
            pltpu.VMEM((height, 8, cells * spec // 8), jnp.float32),
            pltpu.VMEM((spec, levels, cells), jnp.float32),
            pltpu.VMEM((spec, levels, cells + 256), jnp.float32),
        ],
    )(cellhist, rim, weights, jnp.asarray(phit), jnp.asarray(psi))
    return jnp.transpose(lam, (1, 0, 2)), fit


def smooth_levels(field):
    padded = jnp.pad(field, ((0, 0), (1, 1), (0, 0)))
    return 0.5 * field + 0.25 * (padded[:, :-2, :] + padded[:, 2:, :])


def body_inner(hist, dest, cell_in, offsets):
    rows = hist.shape[0]
    width = hist.shape[2]
    cells = offsets.shape[1]
    devices = lax.axis_size(("cell", "own"))
    capacity = 2 * rows // devices
    slots = devices * capacity
    packed = jnp.sum(hist, axis=1, dtype=jnp.float32).astype(jnp.bfloat16)
    target_block = dest[:, 0]
    member = (target_block[:, None] == jnp.arange(devices, dtype=jnp.int32)[None, :]).astype(
        jnp.int32
    )
    ranks = jnp.sum((jnp.cumsum(member, axis=0) - 1) * member, axis=1)
    position = target_block * capacity + ranks
    codes = jnp.stack([cell_in // CODE + 1, cell_in % CODE], axis=1).astype(jnp.bfloat16)
    codes = jnp.pad(codes, ((0, 0), (0, 128 - 2)))
    payload = jnp.concatenate([packed, codes], axis=1)
    place = (jnp.arange(slots, dtype=jnp.int32)[:, None] == position[None, :]).astype(jnp.bfloat16)
    sent = jnp.dot(place, payload, preferred_element_type=jnp.float32)
    narrow = width // SPEC
    halves = [
        sent[:, h * narrow : (h + 1) * narrow].astype(jnp.bfloat16).reshape(devices, capacity, narrow)
        for h in range(SPEC)
    ]
    code_rows = sent[:, width : width + 2].reshape(devices, capacity, 2)
    code_rows = jnp.swapaxes(code_rows, 1, 2).astype(jnp.bfloat16)
    code_rows = jnp.pad(code_rows, ((0, 0), (0, EXTRA - 2), (0, narrow - capacity)))
    message = jnp.concatenate(halves + [code_rows], axis=1)
    got = lax.all_to_all(message, ("cell", "own"), split_axis=0, concat_axis=0, tiled=True)
    recv_halves = [
        got[:, h * capacity : (h + 1) * capacity, :].reshape(slots, narrow) for h in range(SPEC)
    ]
    high = got[:, SPEC * capacity, :capacity].astype(jnp.int32).reshape(slots)
    low = got[:, SPEC * capacity + 1, :capacity].astype(jnp.int32).reshape(slots)
    recv_cells = jnp.where(high > 0, (high - 1) * CODE + low, -1)

    def cell_sums(picked):
        return jnp.stack(
            [
                lax.dot_general(
                    part, picked, (((0,), (0,)), ((), ())), preferred_element_type=jnp.float32
                )
                for part in recv_halves
            ]
        )

    edges = jnp.concatenate(
        [jnp.arange(W, dtype=jnp.int32), jnp.arange(cells - W, cells, dtype=jnp.int32)]
    )
    edge_lev = smooth_levels(cell_sums((recv_cells[:, None] == edges[None, :]).astype(jnp.bfloat16)))
    forward = [(i, i + 1) for i in range(devices - 1)]
    backward = [(target, source) for source, target in forward]
    below = lax.ppermute(edge_lev[:, :, W:], ("cell", "own"), forward)
    above = lax.ppermute(edge_lev[:, :, :W], ("cell", "own"), backward)
    select = (recv_cells[:, None] == jnp.arange(cells, dtype=jnp.int32)[None, :]).astype(
        jnp.bfloat16
    )
    cellhist = cell_sums(select)
    weights = jnp.stack(
        [jnp.sum((offsets == shift).astype(jnp.float32), axis=0) for shift in range(-W, W + 1)]
    )
    rim = jnp.concatenate([below, above], axis=2)
    return fit_all(cellhist, rim, weights, MOM)


def solution(mesh):
    placed = (
        P(("cell", "own"), None, None),
        P(("cell", "own"), None),
        P(("cell", "own")),
        P(None, ("cell", "own")),
    )
    return jax.shard_map(
        body_inner,
        mesh=mesh,
        in_specs=placed,
        out_specs=(P(None, None, ("cell", "own")), P(None, ("cell", "own"))),
        check_vma=False,
    )
```

```python
import jax
import jax.numpy as jnp
import numpy as np
from jax import lax
from jax.experimental import pallas as pl
from jax.experimental.pallas import tpu as pltpu
from jax.sharding import PartitionSpec as P

SPEC = 2
MOM = 6
NEWTON = 8
W = 4
CODE = 32
EXTRA = 8
LOOP_PRECISION = lax.Precision.HIGH


def pair_list(count):
    return [(row, col) for row in range(count) for col in range(row + 1)]


def chol_solve(hess, rhs, count):
    lower = [[None] * count for _ in range(count)]
    for row in range(count):
        for col in range(row + 1):
            total = hess[row][col]
            for inner in range(col):
                total = total - lower[row][inner] * lower[col][inner]
            if row == col:
                lower[row][col] = jnp.sqrt(total)
            else:
                lower[row][col] = total / lower[col][col]
    forward = []
    for row in range(count):
        total = rhs[row]
        for inner in range(row):
            total = total - lower[row][inner] * forward[inner]
        forward.append(total / lower[row][row])
    backward = [None] * count
    for row in reversed(range(count)):
        total = forward[row]
        for inner in range(row + 1, count):
            total = total - lower[inner][row] * backward[inner]
        backward[row] = total / lower[row][row]
    return backward


def newton_step(got, moments, lam, count):
    pairs = pair_list(count)
    norm = got[count]
    first = [got[m] / norm for m in range(count)]
    hess = [[None] * count for _ in range(count)]
    for k, (row, col) in enumerate(pairs):
        second = got[count + 1 + k] / norm
        value = second - first[row] * first[col]
        if row == col:
            value = value + 0.01
        hess[row][col] = value
    rhs = [first[m] - moments[m] for m in range(count)]
    delta = chol_solve(hess, rhs, count)
    return [lam[m] - 0.5 * delta[m] for m in range(count)]


def fit_kernel(
    h_ref, rim_ref, w_ref, phit_ref, psi_ref, lam_ref, fit_ref, lam_s, dense_ref, t_ref, ext_ref
):
    spec, levels, cells = h_ref.shape
    pad = (ext_ref.shape[2] - cells) // 2
    rim = rim_ref.shape[2] // 2
    ext_ref[...] = jnp.zeros(ext_ref.shape, jnp.float32)
    for s in range(spec):
        field = h_ref[s]
        t_ref[s] = field
        lower = jnp.concatenate([jnp.zeros((1, cells), jnp.float32), t_ref[s, : levels - 1, :]], axis=0)
        upper = jnp.concatenate([t_ref[s, 1:, :], jnp.zeros((1, cells), jnp.float32)], axis=0)
        levelled = 0.5 * field + 0.25 * (lower + upper)
        ext_ref[s, :, pad : pad + cells] = levelled
        ext_ref[s, :, pad - rim : pad] = rim_ref[s, :, :rim]
        ext_ref[s, :, pad + cells : pad + cells + rim] = rim_ref[s, :, rim:]
        target = 1.0 + levelled
        for k in range(w_ref.shape[0]):
            shift = k - w_ref.shape[0] // 2
            target = target + w_ref[k : k + 1, :] * ext_ref[s, :, pad + shift : pad + shift + cells]
        t_ref[s] = target
    count = lam_ref.shape[0]
    used = count + 1 + len(pair_list(count))
    groups = 8 // spec
    part = cells // groups
    highest = lax.Precision.HIGHEST

    def contract(a, b, precision=highest):
        return jnp.dot(a, b, precision=precision, preferred_element_type=jnp.float32)

    def densify(gots):
        for s in range(spec):
            for j in range(groups):
                piece = gots[s][:, j * part : (j + 1) * part]
                row = s * groups + j
                for k in range(used):
                    dense_ref[k, row : row + 1, :] = piece[k : k + 1, :]
        return [dense_ref[k] for k in range(used)]

    def spread(values):
        for m in range(count):
            for s in range(spec):
                for j in range(groups):
                    row = s * groups + j
                    lam_s[s, m : m + 1, j * part : (j + 1) * part] = values[m][row : row + 1, :]

    got = densify([contract(psi_ref[...], t_ref[s]) for s in range(spec)])
    moments = [got[m] / got[count] for m in range(count)]
    lam_s[...] = jnp.zeros(lam_s.shape, jnp.float32)
    zero = jnp.zeros((8, part), jnp.float32)

    def step(_, lam):
        gots = []
        for s in range(spec):
            expo = jnp.exp(contract(phit_ref[...], lam_s[s], LOOP_PRECISION))
            gots.append(contract(psi_ref[...], expo, LOOP_PRECISION))
        new = newton_step(densify(gots), moments, list(lam), count)
        spread(new)
        return tuple(new)

    lax.fori_loop(0, NEWTON, step, tuple([zero] * count))
    for s in range(spec):
        target = t_ref[s]
        exponent = contract(phit_ref[...], lam_s[s])
        log_norm = jnp.log(jnp.sum(jnp.exp(exponent), axis=0, keepdims=True))
        whole = jnp.sum(target, axis=0, keepdims=True)
        ratio = jnp.log(target / whole) - (exponent - log_norm)
        fit_ref[s : s + 1, :] = 2.0 * jnp.sum(target * ratio, axis=0, keepdims=True) / levels
        for m in range(count):
            lam_ref[m, s : s + 1, :] = lam_s[s, m : m + 1, :]


def legendre_numpy(levels, count):
    xpos = (2.0 * np.arange(levels, dtype=np.float64) + 1.0) / levels - 1.0
    prev = np.ones_like(xpos)
    curr = xpos
    table = [curr]
    for order in range(1, count):
        nxt = ((2 * order + 1) * xpos * curr - order * prev) / (order + 1)
        prev, curr = (curr, nxt)
        table.append(curr)
    return np.stack(table, axis=0).astype(np.float32)


def fit_all(cellhist, rim, weights, count):
    spec, levels, cells = cellhist.shape
    phi = legendre_numpy(levels, count)
    pairs = pair_list(count)
    width = 8
    phit = np.zeros((levels, width), np.float32)
    phit[:, :count] = phi.T
    rows = [phi[m] for m in range(count)] + [np.ones((levels,), np.float32)]
    rows += [phi[r] * phi[c] for r, c in pairs]
    height = -(-len(rows) // 8) * 8
    rows += [np.zeros((levels,), np.float32)] * (height - len(rows))
    psi = np.stack(rows, axis=0)
    lam, fit = pl.pallas_call(
        fit_kernel,
        out_shape=(
            jax.ShapeDtypeStruct((count, spec, cells), jnp.float32),
            jax.ShapeDtypeStruct((spec, cells), jnp.float32),
        ),
        scratch_shapes=[
            pltpu.VMEM((spec, width, cells), jnp.float32),
            pltpu.VMEM((height, 8, cells * spec // 8), jnp.float32),
            pltpu.VMEM((spec, levels, cells), jnp.float32),
            pltpu.VMEM((spec, levels, cells + 256), jnp.float32),
        ],
    )(cellhist, rim, weights, jnp.asarray(phit), jnp.asarray(psi))
    return jnp.transpose(lam, (1, 0, 2)), fit


def smooth_levels(field):
    padded = jnp.pad(field, ((0, 0), (1, 1), (0, 0)))
    return 0.5 * field + 0.25 * (padded[:, :-2, :] + padded[:, 2:, :])


def body_inner(hist, dest, cell_in, offsets):
    rows = hist.shape[0]
    width = hist.shape[2]
    cells = offsets.shape[1]
    devices = lax.axis_size(("cell", "own"))
    capacity = 2 * rows // devices
    slots = devices * capacity
    packed = jnp.sum(hist, axis=1, dtype=jnp.float32).astype(jnp.bfloat16)
    target_block = dest[:, 0]
    member = (target_block[:, None] == jnp.arange(devices, dtype=jnp.int32)[None, :]).astype(
        jnp.int32
    )
    ranks = jnp.sum((jnp.cumsum(member, axis=0) - 1) * member, axis=1)
    position = target_block * capacity + ranks
    column = jnp.arange(128, dtype=jnp.int32)[None, :]
    codes = jnp.where(
        column == 0, cell_in[:, None] // CODE + 1, jnp.where(column == 1, cell_in[:, None] % CODE, 0)
    ).astype(jnp.bfloat16)
    payload = jnp.concatenate([packed, codes], axis=1)
    place = (jnp.arange(slots, dtype=jnp.int32)[:, None] == position[None, :]).astype(jnp.bfloat16)
    sent = jnp.dot(place, payload, preferred_element_type=jnp.float32)
    narrow = width // SPEC
    halves = [
        sent[:, h * narrow : (h + 1) * narrow].astype(jnp.bfloat16).reshape(devices, capacity, narrow)
        for h in range(SPEC)
    ]
    code_rows = sent[:, width : width + 2].reshape(devices, capacity, 2)
    code_rows = jnp.swapaxes(code_rows, 1, 2).astype(jnp.bfloat16)
    code_rows = jnp.pad(code_rows, ((0, 0), (0, EXTRA - 2), (0, narrow - capacity)))
    message = jnp.concatenate(halves + [code_rows], axis=1)
    got = lax.all_to_all(message, ("cell", "own"), split_axis=0, concat_axis=0, tiled=True)
    recv_halves = [
        got[:, h * capacity : (h + 1) * capacity, :].reshape(slots, narrow) for h in range(SPEC)
    ]
    high = got[:, SPEC * capacity, :capacity].astype(jnp.int32).reshape(slots)
    low = got[:, SPEC * capacity + 1, :capacity].astype(jnp.int32).reshape(slots)
    recv_cells = jnp.where(high > 0, (high - 1) * CODE + low, -1)

    def cell_sums(picked):
        return jnp.stack(
            [
                lax.dot_general(
                    part, picked, (((0,), (0,)), ((), ())), preferred_element_type=jnp.float32
                )
                for part in recv_halves
            ]
        )

    edges = jnp.concatenate(
        [jnp.arange(W, dtype=jnp.int32), jnp.arange(cells - W, cells, dtype=jnp.int32)]
    )
    edge_lev = smooth_levels(cell_sums((recv_cells[:, None] == edges[None, :]).astype(jnp.bfloat16)))
    forward = [(i, i + 1) for i in range(devices - 1)]
    backward = [(target, source) for source, target in forward]
    below = lax.ppermute(edge_lev[:, :, W:], ("cell", "own"), forward)
    above = lax.ppermute(edge_lev[:, :, :W], ("cell", "own"), backward)
    select = (recv_cells[:, None] == jnp.arange(cells, dtype=jnp.int32)[None, :]).astype(
        jnp.bfloat16
    )
    cellhist = cell_sums(select)
    weights = jnp.stack(
        [jnp.sum((offsets == shift).astype(jnp.float32), axis=0) for shift in range(-W, W + 1)]
    )
    rim = jnp.concatenate([below, above], axis=2)
    return fit_all(cellhist, rim, weights, MOM)


def solution(mesh):
    placed = (
        P(("cell", "own"), None, None),
        P(("cell", "own"), None),
        P(("cell", "own")),
        P(None, ("cell", "own")),
    )
    return jax.shard_map(
        body_inner,
        mesh=mesh,
        in_specs=placed,
        out_specs=(P(None, None, ("cell", "own")), P(None, ("cell", "own"))),
        check_vma=False,
    )
```
